128 devices in a mesh: dp: 4 (over z), seq: 32 (over y, x, core).
Axes of the slice: x: 4, y: 4, z: 4, core: 2. Of those that a mesh axis runs over, the one named last changes fastest.
Arguments:
- queries: bfloat16 [49152, 2048], P(('dp', 'seq')), parts along dimension 0, may hold values from -6 to 6
- keys_in: bfloat16 [49152, 2048], P(('dp', 'seq')), parts along dimension 0, may hold values from -6 to 6
- values: bfloat16 [49152, 2048], P(('dp', 'seq')), parts along dimension 0, may hold values from -6 to 6
- stream: bfloat16 [49152, 2048], P(('dp', 'seq')), parts along dimension 0, may hold values from -6 to 6
- log_decay: float32 [49152, 16], P(('dp', 'seq')), parts along dimension 0, may hold values from -1 to 0
- token_index: int32 [128, 768], P('dp', 'seq'), parts along dimension 0, may hold values from 0 to 12287, as said below
- route_weight: float32 [128, 768], P('dp', 'seq'), parts along dimension 0, may hold values from 0.2 to 1
- moe_gain: float32 [2048], replicated, may hold values from 0.25 to 1.75
- out_weight: bfloat16 [2048, 2048], P('seq'), may hold values from -0.125 to 0.125
- gate_weight: bfloat16 [32, 2048, 1408], P('seq'), may hold values from -0.125 to 0.125
- up_weight: bfloat16 [32, 2048, 1408], P('seq'), may hold values from -0.125 to 0.125
- down_weight: bfloat16 [32, 1408, 2048], P('seq'), may hold values from -0.15625 to 0.15625
Outputs:
- mixed: bfloat16 [49152, 2048], P(('dp', 'seq')), parts along dimension 0
The draws below stay inside these ranges and needn't reach their ends.
There are 4 independent parts, one for each index of `dp`. The reference program is written for one: setup_inputs(seed, part) draws one part's arguments, and reference() takes and returns one part's arrays. A program takes and returns all parts, laid end to end along the dimension named above; an argument that names none is the same for every part. Nothing has to cross between parts.
Inputs may be any that keep to these rules, and one draw needn't show every extreme that they name: `token_index`: for each expert and each j, positions j * 24 to (j + 1) * 24 - 1 of its row hold 24 different tokens of the j-th block of 384 tokens, in ascending order.
All inputs are finite; a program needn't handle non-finite values.
Results may differ from the reference program's by a relative error of at most 0.014.
Values may be sent and summed in bfloat16 or wider, within the bound.
No kernel may reach another device: no remote copies, remote signals or barrier semaphores. Data moves between devices by JAX's collectives and lax.ppermute only.
A program may use at most 192 MiB of HBM per device.

```python
import math
import jax
import jax.numpy as jnp
from jax import lax

D = 2048
H = 16
DH = 128
FF = 1408
TOK_DEV = 384
SPAN_TOKENS = 12288
EXPERTS = 32
CAP = 768
PER_SRC = 24


def draw_log_decay(key, part):
    segment_parts = jax.random.split(key, 9)
    blocks = SPAN_TOKENS // TOK_DEV
    forget_count = max(1, H // 2)
    ranking = jax.random.permutation(segment_parts[0], H)
    forgetting = ranking < forget_count
    block_strength = jnp.exp(jax.random.uniform(segment_parts[1], (blocks, H), minval=math.log(0.2), maxval=math.log(12.0))) / TOK_DEV
    keep_rate = jnp.exp(jax.random.uniform(segment_parts[2], (H,), minval=math.log(0.02), maxval=math.log(0.1))) / SPAN_TOKENS
    keep_factor = jnp.exp(jax.random.uniform(segment_parts[3], (blocks, H), minval=math.log(0.6), maxval=math.log(1.8)))
    raised_block = jax.random.randint(segment_parts[4], (H,), 0, blocks)
    raised_amount = jnp.exp(jax.random.uniform(segment_parts[5], (H,), minval=math.log(0.35), maxval=math.log(0.6))) / TOK_DEV
    block_numbers = jnp.arange(blocks)
    keep_strength = keep_rate[None, :] * keep_factor + jnp.where(block_numbers[:, None] == raised_block[None, :], raised_amount[None, :], 0.0)
    strength = jnp.where(forgetting[None, :], block_strength, keep_strength)
    position_factor = jax.random.uniform(segment_parts[6], (SPAN_TOKENS, H), minval=0.5, maxval=1.5)
    token_values = jnp.minimum(jnp.repeat(strength, TOK_DEV, axis=0) * position_factor, 0.3)
    segment_start = jax.random.randint(segment_parts[7], (2,), 0, SPAN_TOKENS)
    segment_length = jax.random.uniform(segment_parts[8], (2,), minval=math.log(0.5), maxval=math.log(0.8))
    token_places = jnp.arange(SPAN_TOKENS)
    segment_list = jnp.where(token_places == segment_start[0], segment_length[0], 0.0) + jnp.where(token_places == segment_start[1], segment_length[1], 0.0)
    combined_output = -token_values + segment_list[:, None]
    return combined_output.astype(jnp.float32)


def draw_token_index(key, part):
    sources = SPAN_TOKENS // TOK_DEV
    streams = jax.random.split(key, EXPERTS * sources)
    shuffled = jax.vmap(lambda single: jax.random.permutation(single, TOK_DEV))(streams)
    chosen = jnp.sort(shuffled[:, :PER_SRC], axis=1).reshape(EXPERTS, sources, PER_SRC)
    chosen = chosen + (jnp.arange(sources) * TOK_DEV)[None, :, None]
    return chosen.reshape(EXPERTS, CAP).astype(jnp.int32)


def block_scale(own_key, dims, shards, least, largest):
    level, own = 1.0, jax.random.fold_in(own_key, 6)
    for position, shards_of in shards:
        steps = jnp.exp(jax.random.uniform(jax.random.fold_in(own, position), (shards_of,), jnp.float32, least / len(shards), largest / len(shards)))
        level = level * jnp.repeat(steps, dims[position] // shards_of).reshape([-1 if axis == position else 1 for axis in range(len(dims))])
    return level


def normal_values(rng, shape, scale, bound, cuts=(), dtype=jnp.bfloat16):
    entries = scale * jax.random.normal(rng, shape, jnp.float32)
    if cuts:
        entries = entries * block_scale(rng, shape, cuts, -0.22, 0.18)
    return jnp.clip(entries, -bound, bound).astype(dtype)


def setup_inputs(seed: int = 0, part: int = 0) -> dict:
    seeds = jax.random.split(jax.random.key(seed), 13)
    part_keys = jax.random.split(jax.random.fold_in(seeds[12], part), 13)
    queries = normal_values(part_keys[0], (SPAN_TOKENS, D), 1.0, 6.0, ((0, 32),))
    keys_in = normal_values(part_keys[1], (SPAN_TOKENS, D), 1.0, 6.0, ((0, 32),))
    values = normal_values(part_keys[2], (SPAN_TOKENS, D), 1.0, 6.0, ((0, 32),))
    stream = normal_values(part_keys[3], (SPAN_TOKENS, D), 1.0, 6.0, ((0, 32),))
    log_decay = draw_log_decay(jax.random.fold_in(jax.random.fold_in(seeds[12], part), 71), part)
    token_index = draw_token_index(jax.random.fold_in(jax.random.fold_in(seeds[12], part), 71), part)
    route_weight = jnp.clip(0.2 + 0.8 * jax.random.uniform(part_keys[6], (EXPERTS, CAP), jnp.float32) ** block_scale(part_keys[6], (EXPERTS, CAP), ((1, 32),), -0.2, 0.2), 0.2, 1.0)
    moe_gain = jnp.clip(1.0 + 0.15 * jax.random.normal(seeds[7], (D,), jnp.float32), 0.25, 1.75)
    out_weight = normal_values(seeds[8], (D, D), D ** -0.5, 0.125, ((0, 32),))
    gate_weight = normal_values(seeds[9], (EXPERTS, D, FF), D ** -0.5, 0.125, ((0, 32),))
    up_weight = normal_values(seeds[10], (EXPERTS, D, FF), D ** -0.5, 0.125, ((0, 32),))
    down_weight = normal_values(seeds[11], (EXPERTS, FF, D), FF ** -0.5, 0.15625, ((0, 32),))
    return {"queries": queries, "keys_in": keys_in, "values": values, "stream": stream, "log_decay": log_decay, "token_index": token_index, "route_weight": route_weight, "moe_gain": moe_gain, "out_weight": out_weight, "gate_weight": gate_weight, "up_weight": up_weight, "down_weight": down_weight}


def reference(queries, keys_in, values, stream, log_decay, token_index, route_weight, moe_gain, out_weight, gate_weight, up_weight, down_weight):
    blocks = SPAN_TOKENS // TOK_DEV
    scaling = DH ** (-0.5)
    highest = lax.Precision.HIGHEST
    query_blocks = queries.reshape(blocks, TOK_DEV, H, DH)
    key_blocks = keys_in.reshape(blocks, TOK_DEV, H, DH)
    value_blocks = values.reshape(blocks, TOK_DEV, H, DH)
    decay_blocks = log_decay.reshape(blocks, TOK_DEV, H)
    causal = jnp.arange(TOK_DEV)[:, None] >= jnp.arange(TOK_DEV)[None, :]

    def one_block(carried, inputs):
        query_part, key_part, value_part, decay_part = inputs
        running = jnp.cumsum(decay_part, axis=0)
        ending = running[-1]
        spacing = running[:, None, :] - running[None, :, :]
        decay_mask = jnp.where(causal[:, :, None], jnp.exp(jnp.minimum(spacing, 0.0)), 0.0)
        query_wide = query_part.astype(jnp.float32)
        key_wide = key_part.astype(jnp.float32)
        value_wide = value_part.astype(jnp.float32)
        scores = (jnp.einsum('thd,shd->tsh', query_wide, key_wide, precision=highest) * scaling * decay_mask).astype(jnp.bfloat16)
        within = jnp.einsum('tsh,shd->thd', lax.optimization_barrier(scores).astype(jnp.float32), value_wide, precision=highest)
        query_scaled = (query_wide * (jnp.exp(running) * scaling)[:, :, None]).astype(jnp.bfloat16)
        state_low = carried.astype(jnp.bfloat16)
        across = jnp.einsum('thd,hde->the', lax.optimization_barrier(query_scaled).astype(jnp.float32), lax.optimization_barrier(state_low).astype(jnp.float32), precision=highest)
        key_scaled = (key_wide * jnp.exp(ending[None, :] - running)[:, :, None]).astype(jnp.bfloat16)
        local_state = jnp.einsum('shd,she->hde', lax.optimization_barrier(key_scaled).astype(jnp.float32), value_wide, precision=highest)
        following = carried * jnp.exp(ending)[:, None, None] + local_state
        return (following, within + across)
    initial = jnp.zeros((H, DH, DH), jnp.float32)
    _, attention = lax.scan(one_block, initial, (query_blocks, key_blocks, value_blocks, decay_blocks))
    attention = attention.reshape(SPAN_TOKENS, H, DH)
    spread = lax.optimization_barrier(jnp.mean(attention * attention, axis=2, keepdims=True))
    normed = (attention * lax.rsqrt(spread + 1e-06)).astype(jnp.bfloat16).reshape(SPAN_TOKENS, D)
    attended = jnp.dot(normed, out_weight, preferred_element_type=jnp.float32)
    residual = (stream.astype(jnp.float32) + attended).astype(jnp.bfloat16)
    widened = residual.astype(jnp.float32)
    mixed_in = (widened * lax.rsqrt(lax.optimization_barrier(jnp.mean(widened * widened, axis=1, keepdims=True)) + 1e-06) * moe_gain).astype(jnp.bfloat16)

    def one_expert(inputs):
        chosen, gating_w, upward_w, downward_w = inputs
        picked = jnp.take(mixed_in, chosen, axis=0).astype(jnp.float32)
        gating = jnp.dot(picked, gating_w.astype(jnp.float32), precision=highest)
        upward = jnp.dot(picked, upward_w.astype(jnp.float32), precision=highest)
        activated = (jax.nn.silu(gating) * upward).astype(jnp.bfloat16)
        product = jnp.dot(lax.optimization_barrier(activated).astype(jnp.float32), downward_w.astype(jnp.float32), precision=highest)
        return product.astype(jnp.bfloat16)
    expert_out = lax.map(one_expert, (token_index, gate_weight, up_weight, down_weight))
    weighted = expert_out.astype(jnp.float32) * route_weight[:, :, None]
    total = widened.at[token_index.reshape(-1)].add(weighted.reshape(-1, D))
    return total.astype(jnp.bfloat16)
```

```python
import jax
import jax.numpy as jnp
from jax import lax
from jax.sharding import PartitionSpec as P


def carried_in(state, ending, axis):
    count = lax.axis_size(axis)

    def shifted(part, distance):
        pairs = [(j, j + distance) for j in range(count - distance)]
        return lax.ppermute(part, axis, pairs)

    def combine(earlier, latter):
        return (earlier[0] * jnp.exp(latter[1])[:, None, None] + latter[0], earlier[1] + latter[1])

    def fetch(pair, distance):
        low, wide = pair
        return (shifted(low.astype(jnp.bfloat16), distance).astype(jnp.float32), shifted(wide, distance))

    covered = (state, ending)
    reach = 1
    while 2 * reach < count:
        covered = combine(fetch(covered, reach), covered)
        reach *= 2
    if count == 1:
        return jnp.zeros_like(state)
    near = fetch(covered, 1)
    if reach + 1 < count:
        near = combine(fetch(covered, reach + 1), near)
    return near[0]


def shards(
    queries,
    keys_in,
    values,
    stream,
    log_decay,
    token_index,
    route_weight,
    moe_gain,
    out_weight,
    gate_weight,
    up_weight,
    down_weight,
):
    length, model_width = queries.shape
    head_count = log_decay.shape[1]
    head_size = model_width // head_count
    scaling = head_size ** (-0.5)
    device = lax.axis_index("seq")
    query_heads = queries.reshape(length, head_count, head_size)
    key_heads = keys_in.reshape(length, head_count, head_size)
    value_heads = values.reshape(length, head_count, head_size)
    running = jnp.cumsum(log_decay, axis=0)
    ending = running[-1]
    shrink = jnp.exp(ending[None, :] - running)
    key_scaled = (key_heads.astype(jnp.float32) * shrink[:, :, None]).astype(jnp.bfloat16)
    local_state = jnp.einsum(
        "shd,she->hde", key_scaled, value_heads, preferred_element_type=jnp.float32
    )
    incoming = carried_in(local_state, ending, "seq")
    scores = (
        jnp.einsum("thd,shd->hts", query_heads, key_heads, preferred_element_type=jnp.float32)
        * scaling
    )
    spacing = running.T[:, :, None] - running.T[:, None, :]
    causal = jnp.arange(length)[:, None] >= jnp.arange(length)[None, :]
    decay_mask = jnp.where(causal[None], jnp.exp(jnp.minimum(spacing, 0.0)), 0.0)
    attend_weights = (scores * decay_mask).astype(jnp.bfloat16)
    within = jnp.einsum(
        "hts,shd->thd", attend_weights, value_heads, preferred_element_type=jnp.float32
    )
    query_scaled = (
        query_heads.astype(jnp.float32) * (jnp.exp(running) * scaling)[:, :, None]
    ).astype(jnp.bfloat16)
    across = jnp.einsum(
        "thd,hde->the",
        query_scaled,
        incoming.astype(jnp.bfloat16),
        preferred_element_type=jnp.float32,
    )
    unnormed = within + across
    spread = jnp.mean(unnormed * unnormed, axis=2, keepdims=True)
    normed = (
        (unnormed * lax.rsqrt(spread + 1e-06)).astype(jnp.bfloat16).reshape(length, model_width)
    )
    attended = jnp.dot(
        normed,
        lax.all_gather(out_weight, "seq", axis=0, tiled=True),
        preferred_element_type=jnp.float32,
    )
    residual = (stream.astype(jnp.float32) + attended).astype(jnp.bfloat16)
    widened = residual.astype(jnp.float32)
    mixed_in = (
        widened * lax.rsqrt(jnp.mean(widened * widened, axis=1, keepdims=True) + 1e-06) * moe_gain
    ).astype(jnp.bfloat16)
    offsets = token_index - device * length
    picked = jnp.take(mixed_in, offsets, axis=0)
    arrived = lax.all_to_all(picked, "seq", split_axis=0, concat_axis=0, tiled=True)
    gating = jnp.einsum("snd,df->snf", arrived, gate_weight[0], preferred_element_type=jnp.float32)
    upward = jnp.einsum("snd,df->snf", arrived, up_weight[0], preferred_element_type=jnp.float32)
    activated = (jax.nn.silu(gating) * upward).astype(jnp.bfloat16)
    produced = jnp.einsum(
        "snf,fd->snd", activated, down_weight[0], preferred_element_type=jnp.float32
    ).astype(jnp.bfloat16)
    returned = lax.all_to_all(produced, "seq", split_axis=0, concat_axis=0, tiled=True)
    scaled = returned.astype(jnp.float32) * route_weight[:, :, None]
    total = widened.at[offsets.reshape(-1)].add(scaled.reshape(-1, model_width))
    return total.astype(jnp.bfloat16)


def solution(mesh):
    placed = (
        P(("dp", "seq"), None),
        P(("dp", "seq"), None),
        P(("dp", "seq"), None),
        P(("dp", "seq"), None),
        P(("dp", "seq"), None),
        P("dp", "seq"),
        P("dp", "seq"),
        P(),
        P("seq", None),
        P("seq", None, None),
        P("seq", None, None),
        P("seq", None, None),
    )
    return jax.shard_map(
        shards, mesh=mesh, in_specs=placed, out_specs=P(("dp", "seq"), None), check_vma=False
    )
```

```python
import jax
import jax.numpy as jnp
from jax import lax
from jax.sharding import PartitionSpec as P


def carried_in(state, ending, axis):
    count = lax.axis_size(axis)

    def shifted(part, distance):
        pairs = [(j, j + distance) for j in range(count - distance)]
        return lax.ppermute(part, axis, pairs)

    def combine(earlier, latter):
        return (earlier[0] * jnp.exp(latter[1])[:, None, None] + latter[0], earlier[1] + latter[1])

    heads, rows, width = state.shape

    def pieces(wide):
        parts = []
        for _ in range(3):
            part = wide.astype(jnp.bfloat16)
            parts.append(part)
            wide = wide - part.astype(jnp.float32)
        block = jnp.stack(parts, axis=1)
        return jnp.pad(block, ((0, 0), (0, width - 3)))

    def fetch(pair, distance):
        low, wide = pair
        message = jnp.concatenate(
            [low.astype(jnp.bfloat16).reshape(heads * rows, width), pieces(wide)], axis=0
        )
        arrived = shifted(message, distance)
        body = arrived[: heads * rows].reshape(heads, rows, width).astype(jnp.float32)
        tail = arrived[heads * rows :, :3].astype(jnp.float32)
        return (body, tail[:, 0] + tail[:, 1] + tail[:, 2])

    covered = (state, ending)
    reach = 1
    while 2 * reach < count:
        covered = combine(fetch(covered, reach), covered)
        reach *= 2
    if count == 1:
        return jnp.zeros_like(state)
    near = fetch(covered, 1)
    if reach + 1 < count:
        near = combine(fetch(covered, reach + 1), near)
    return near[0]


def shards(
    queries,
    keys_in,
    values,
    stream,
    log_decay,
    token_index,
    route_weight,
    moe_gain,
    out_weight,
    gate_weight,
    up_weight,
    down_weight,
):
    length, model_width = queries.shape
    head_count = log_decay.shape[1]
    head_size = model_width // head_count
    scaling = head_size ** (-0.5)
    device = lax.axis_index("seq")
    query_heads = queries.reshape(length, head_count, head_size)
    key_heads = keys_in.reshape(length, head_count, head_size)
    value_heads = values.reshape(length, head_count, head_size)
    running = jnp.cumsum(log_decay, axis=0)
    ending = running[-1]
    shrink = jnp.exp(ending[None, :] - running)
    key_scaled = (key_heads.astype(jnp.float32) * shrink[:, :, None]).astype(jnp.bfloat16)
    local_state = jnp.einsum(
        "shd,she->hde", key_scaled, value_heads, preferred_element_type=jnp.float32
    )
    incoming = carried_in(local_state, ending, "seq")
    scores = (
        jnp.einsum("thd,shd->hts", query_heads, key_heads, preferred_element_type=jnp.float32)
        * scaling
    )
    spacing = running.T[:, :, None] - running.T[:, None, :]
    causal = jnp.arange(length)[:, None] >= jnp.arange(length)[None, :]
    decay_mask = jnp.where(causal[None], jnp.exp(jnp.minimum(spacing, 0.0)), 0.0)
    attend_weights = (scores * decay_mask).astype(jnp.bfloat16)
    within = jnp.einsum(
        "hts,shd->thd", attend_weights, value_heads, preferred_element_type=jnp.float32
    )
    query_scaled = (
        query_heads.astype(jnp.float32) * (jnp.exp(running) * scaling)[:, :, None]
    ).astype(jnp.bfloat16)
    across = jnp.einsum(
        "thd,hde->the",
        query_scaled,
        incoming.astype(jnp.bfloat16),
        preferred_element_type=jnp.float32,
    )
    unnormed = within + across
    spread = jnp.mean(unnormed * unnormed, axis=2, keepdims=True)
    normed = (
        (unnormed * lax.rsqrt(spread + 1e-06)).astype(jnp.bfloat16).reshape(length, model_width)
    )
    attended = jnp.dot(
        normed,
        lax.all_gather(out_weight, "seq", axis=0, tiled=True),
        preferred_element_type=jnp.float32,
    )
    residual = (stream.astype(jnp.float32) + attended).astype(jnp.bfloat16)
    widened = residual.astype(jnp.float32)
    mixed_in = (
        widened * lax.rsqrt(jnp.mean(widened * widened, axis=1, keepdims=True) + 1e-06) * moe_gain
    ).astype(jnp.bfloat16)
    offsets = (token_index - device * length).reshape(-1)
    positions = jnp.arange(length)
    choose = (offsets[:, None] == positions[None, :]).astype(jnp.bfloat16)
    picked = jnp.dot(choose, mixed_in, preferred_element_type=jnp.float32).astype(jnp.bfloat16)
    picked = picked.reshape(token_index.shape + (model_width,))
    arrived = lax.all_to_all(picked, "seq", split_axis=0, concat_axis=0, tiled=True)
    gating = jnp.einsum("snd,df->snf", arrived, gate_weight[0], preferred_element_type=jnp.float32)
    upward = jnp.einsum("snd,df->snf", arrived, up_weight[0], preferred_element_type=jnp.float32)
    activated = (jax.nn.silu(gating) * upward).astype(jnp.bfloat16)
    produced = jnp.einsum(
        "snf,fd->snd", activated, down_weight[0], preferred_element_type=jnp.float32
    ).astype(jnp.bfloat16)
    returned = lax.all_to_all(produced, "seq", split_axis=0, concat_axis=0, tiled=True)
    spread_weight = jnp.where(
        positions[:, None] == offsets[None, :], route_weight.reshape(-1)[None, :], 0.0
    )
    flat_returned = returned.reshape(-1, model_width)
    total = widened
    for _ in range(3):
        part = spread_weight.astype(jnp.bfloat16)
        total = total + jnp.dot(part, flat_returned, preferred_element_type=jnp.float32)
        spread_weight = spread_weight - part.astype(jnp.float32)
    return total.astype(jnp.bfloat16)


def solution(mesh):
    placed = (
        P(("dp", "seq"), None),
        P(("dp", "seq"), None),
        P(("dp", "seq"), None),
        P(("dp", "seq"), None),
        P(("dp", "seq"), None),
        P("dp", "seq"),
        P("dp", "seq"),
        P(),
        P("seq", None),
        P("seq", None, None),
        P("seq", None, None),
        P("seq", None, None),
    )
    return jax.shard_map(
        shards, mesh=mesh, in_specs=placed, out_specs=P(("dp", "seq"), None), check_vma=False
    )
```

```python
import jax
import jax.numpy as jnp
from jax import lax
from jax.sharding import PartitionSpec as P

SEQ = ("sy", "sx", "sc")
CHIP_AXES = ("sy", "sx")
CORE_AXIS = "sc"


def carried_in(state, ending, axis):
    count = lax.axis_size(axis)

    def shifted(part, distance):
        pairs = [(j, j + distance) for j in range(count - distance)]
        return lax.ppermute(part, axis, pairs)

    def combine(earlier, latter):
        return (earlier[0] * jnp.exp(latter[1])[:, None, None] + latter[0], earlier[1] + latter[1])

    heads, rows, width = state.shape

    def pieces(wide):
        parts = []
        for _ in range(3):
            part = lax.reduce_precision(wide, exponent_bits=8, mantissa_bits=7)
            parts.append(part.astype(jnp.bfloat16))
            wide = wide - part
        block = jnp.stack(parts, axis=1)
        return jnp.pad(block, ((0, 0), (0, width - 3)))

    def fetch(pair, distance):
        low, wide = pair
        message = jnp.concatenate(
            [low.astype(jnp.bfloat16).reshape(heads * rows, width), pieces(wide)], axis=0
        )
        arrived = shifted(message, distance)
        body = arrived[: heads * rows].reshape(heads, rows, width).astype(jnp.float32)
        tail = arrived[heads * rows :, :3].astype(jnp.float32)
        return (body, tail[:, 0] + tail[:, 1] + tail[:, 2])

    covered = (state, ending)
    reach = 1
    while 2 * reach < count:
        covered = combine(fetch(covered, reach), covered)
        reach *= 2
    if count == 1:
        return jnp.zeros_like(state)
    near = fetch(covered, 1)
    if reach + 1 < count:
        near = combine(fetch(covered, reach + 1), near)
    return near[0]


def shards(
    queries,
    keys_in,
    values,
    stream,
    log_decay,
    token_index,
    route_weight,
    moe_gain,
    out_weight,
    gate_weight,
    up_weight,
    down_weight,
):
    length, model_width = queries.shape
    head_count = log_decay.shape[1]
    head_size = model_width // head_count
    scaling = head_size ** (-0.5)
    device = lax.axis_index(SEQ)
    query_heads = queries.reshape(length, head_count, head_size)
    key_heads = keys_in.reshape(length, head_count, head_size)
    value_heads = values.reshape(length, head_count, head_size)
    running = jnp.cumsum(log_decay, axis=0)
    ending = running[-1]
    shrink = jnp.exp(ending[None, :] - running)
    key_scaled = (key_heads.astype(jnp.float32) * shrink[:, :, None]).astype(jnp.bfloat16)
    local_state = jnp.einsum(
        "shd,she->hde", key_scaled, value_heads, preferred_element_type=jnp.float32
    )
    incoming = carried_in(local_state, ending, SEQ)
    scores = (
        jnp.einsum("thd,shd->hts", query_heads, key_heads, preferred_element_type=jnp.float32)
        * scaling
    )
    spacing = running.T[:, :, None] - running.T[:, None, :]
    causal = jnp.arange(length)[:, None] >= jnp.arange(length)[None, :]
    decay_mask = jnp.where(causal[None], jnp.exp(jnp.minimum(spacing, 0.0)), 0.0)
    attend_weights = (scores * decay_mask).astype(jnp.bfloat16)
    within = jnp.einsum(
        "hts,shd->thd", attend_weights, value_heads, preferred_element_type=jnp.float32
    )
    query_scaled = (
        query_heads.astype(jnp.float32) * (jnp.exp(running) * scaling)[:, :, None]
    ).astype(jnp.bfloat16)
    across = jnp.einsum(
        "thd,hde->the",
        query_scaled,
        incoming.astype(jnp.bfloat16),
        preferred_element_type=jnp.float32,
    )
    unnormed = within + across
    spread = jnp.mean(unnormed * unnormed, axis=2, keepdims=True)
    normed = (
        (unnormed * lax.rsqrt(spread + 1e-06)).astype(jnp.bfloat16).reshape(length, model_width)
    )
    chips = lax.all_gather(out_weight, CHIP_AXES, axis=0, tiled=True)
    gathered = lax.all_gather(chips, CORE_AXIS, axis=0)
    cores = gathered.shape[0]
    attended = jnp.einsum(
        "tcbr,bcrd->td",
        normed.reshape(length, -1, cores, out_weight.shape[0]),
        gathered.reshape(cores, -1, out_weight.shape[0], model_width),
        preferred_element_type=jnp.float32,
    )
    residual = (stream.astype(jnp.float32) + attended).astype(jnp.bfloat16)
    widened = residual.astype(jnp.float32)
    mixed_in = (
        widened * lax.rsqrt(jnp.mean(widened * widened, axis=1, keepdims=True) + 1e-06) * moe_gain
    ).astype(jnp.bfloat16)
    offsets = (token_index - device * length).reshape(-1)
    positions = jnp.arange(length)
    choose = (offsets[:, None] == positions[None, :]).astype(jnp.bfloat16)
    picked = jnp.dot(choose, mixed_in, preferred_element_type=jnp.float32).astype(jnp.bfloat16)
    picked = picked.reshape(token_index.shape + (model_width,))
    arrived = lax.all_to_all(picked, SEQ, split_axis=0, concat_axis=0, tiled=True)
    gating = jnp.einsum("snd,df->snf", arrived, gate_weight[0], preferred_element_type=jnp.float32)
    upward = jnp.einsum("snd,df->snf", arrived, up_weight[0], preferred_element_type=jnp.float32)
    activated = (jax.nn.silu(gating) * upward).astype(jnp.bfloat16)
    produced = jnp.einsum(
        "snf,fd->snd", activated, down_weight[0], preferred_element_type=jnp.float32
    ).astype(jnp.bfloat16)
    returned = lax.all_to_all(produced, SEQ, split_axis=0, concat_axis=0, tiled=True)
    spread_weight = jnp.where(
        positions[:, None] == offsets[None, :], route_weight.reshape(-1)[None, :], 0.0
    )
    flat_returned = returned.reshape(-1, model_width)
    total = widened
    for _ in range(3):
        part = lax.reduce_precision(spread_weight, exponent_bits=8, mantissa_bits=7)
        total = total + jnp.dot(
            part.astype(jnp.bfloat16), flat_returned, preferred_element_type=jnp.float32
        )
        spread_weight = spread_weight - part
    return total.astype(jnp.bfloat16)


def solution(mesh):
    fine = jax.sharding.Mesh(
        mesh.devices.reshape(mesh.shape["dp"], 4, -1, 2),
        ("dp",) + SEQ,
    )
    placed = (
        P(("dp",) + SEQ, None),
        P(("dp",) + SEQ, None),
        P(("dp",) + SEQ, None),
        P(("dp",) + SEQ, None),
        P(("dp",) + SEQ, None),
        P("dp", SEQ),
        P("dp", SEQ),
        P(),
        P(SEQ, None),
        P(SEQ, None, None),
        P(SEQ, None, None),
        P(SEQ, None, None),
    )
    return jax.shard_map(
        shards, mesh=fine, in_specs=placed, out_specs=P(("dp",) + SEQ, None), check_vma=False
    )
```

```python
import jax
import jax.numpy as jnp
from jax import lax
from jax.sharding import PartitionSpec as P

SEQ = ("sy", "sx", "sc")
CHIP_AXES = ("sy", "sx")
CORE_AXIS = "sc"
CHUNKS = 2


def carried_in(state, ending, axis):
    count = lax.axis_size(axis)

    def shifted(part, distance):
        pairs = [(j, j + distance) for j in range(count - distance)]
        return lax.ppermute(part, axis, pairs)

    def combine(earlier, latter):
        return (earlier[0] * jnp.exp(latter[1])[:, None, None] + latter[0], earlier[1] + latter[1])

    heads, rows, width = state.shape

    def pieces(wide):
        parts = []
        for _ in range(3):
            part = lax.reduce_precision(wide, exponent_bits=8, mantissa_bits=7)
            parts.append(part.astype(jnp.bfloat16))
            wide = wide - part
        block = jnp.stack(parts, axis=1)
        return jnp.pad(block, ((0, 0), (0, width - 3)))

    def fetch(pair, distance):
        low, wide = pair
        message = jnp.concatenate(
            [low.astype(jnp.bfloat16).reshape(heads * rows, width), pieces(wide)], axis=0
        )
        arrived = shifted(message, distance)
        body = arrived[: heads * rows].reshape(heads, rows, width).astype(jnp.float32)
        tail = arrived[heads * rows :, :3].astype(jnp.float32)
        return (body, tail[:, 0] + tail[:, 1] + tail[:, 2])

    covered = (state, ending)
    reach = 1
    while 2 * reach < count:
        covered = combine(fetch(covered, reach), covered)
        reach *= 2
    if count == 1:
        return jnp.zeros_like(state)
    near = fetch(covered, 1)
    if reach + 1 < count:
        near = combine(fetch(covered, reach + 1), near)
    return near[0]


def shards(
    queries,
    keys_in,
    values,
    stream,
    log_decay,
    token_index,
    route_weight,
    moe_gain,
    out_weight,
    gate_weight,
    up_weight,
    down_weight,
):
    length, model_width = queries.shape
    head_count = log_decay.shape[1]
    head_size = model_width // head_count
    scaling = head_size ** (-0.5)
    device = lax.axis_index(SEQ)
    query_heads = queries.reshape(length, head_count, head_size)
    key_heads = keys_in.reshape(length, head_count, head_size)
    value_heads = values.reshape(length, head_count, head_size)
    running = jnp.cumsum(log_decay, axis=0)
    ending = running[-1]
    shrink = jnp.exp(ending[None, :] - running)
    key_scaled = (key_heads.astype(jnp.float32) * shrink[:, :, None]).astype(jnp.bfloat16)
    local_state = jnp.einsum(
        "shd,she->hde", key_scaled, value_heads, preferred_element_type=jnp.float32
    )
    incoming = carried_in(local_state, ending, SEQ)
    scores = (
        jnp.einsum("thd,shd->hts", query_heads, key_heads, preferred_element_type=jnp.float32)
        * scaling
    )
    spacing = running.T[:, :, None] - running.T[:, None, :]
    causal = jnp.arange(length)[:, None] >= jnp.arange(length)[None, :]
    decay_mask = jnp.where(causal[None], jnp.exp(jnp.minimum(spacing, 0.0)), 0.0)
    attend_weights = (scores * decay_mask).astype(jnp.bfloat16)
    within = jnp.einsum(
        "hts,shd->thd", attend_weights, value_heads, preferred_element_type=jnp.float32
    )
    query_scaled = (
        query_heads.astype(jnp.float32) * (jnp.exp(running) * scaling)[:, :, None]
    ).astype(jnp.bfloat16)
    across = jnp.einsum(
        "thd,hde->the",
        query_scaled,
        incoming.astype(jnp.bfloat16),
        preferred_element_type=jnp.float32,
    )
    unnormed = within + across
    spread = jnp.mean(unnormed * unnormed, axis=2, keepdims=True)
    normed = (
        (unnormed * lax.rsqrt(spread + 1e-06)).astype(jnp.bfloat16).reshape(length, model_width)
    )
    attended = jnp.dot(
        normed,
        lax.all_gather(out_weight, SEQ, axis=0, tiled=True),
        preferred_element_type=jnp.float32,
    )
    residual = (stream.astype(jnp.float32) + attended).astype(jnp.bfloat16)
    widened = residual.astype(jnp.float32)
    mixed_in = (
        widened * lax.rsqrt(jnp.mean(widened * widened, axis=1, keepdims=True) + 1e-06) * moe_gain
    ).astype(jnp.bfloat16)
    offsets = (token_index - device * length).reshape(-1)
    positions = jnp.arange(length)
    choose = (offsets[:, None] == positions[None, :]).astype(jnp.bfloat16)
    picked = jnp.dot(choose, mixed_in, preferred_element_type=jnp.float32).astype(jnp.bfloat16)
    picked = picked.reshape(token_index.shape + (model_width,))
    spread_weight = jnp.where(
        positions[:, None] == offsets[None, :], route_weight.reshape(-1)[None, :], 0.0
    ).reshape((length,) + token_index.shape)
    slots = token_index.shape[1]
    step = slots // CHUNKS
    total = widened
    for chunk in range(CHUNKS):
        window = slice(chunk * step, (chunk + 1) * step)
        arrived = lax.all_to_all(picked[:, window], SEQ, split_axis=0, concat_axis=0, tiled=True)
        gating = jnp.einsum(
            "snd,df->snf", arrived, gate_weight[0], preferred_element_type=jnp.float32
        )
        upward = jnp.einsum("snd,df->snf", arrived, up_weight[0], preferred_element_type=jnp.float32)
        activated = (jax.nn.silu(gating) * upward).astype(jnp.bfloat16)
        produced = jnp.einsum(
            "snf,fd->snd", activated, down_weight[0], preferred_element_type=jnp.float32
        ).astype(jnp.bfloat16)
        returned = lax.all_to_all(produced, SEQ, split_axis=0, concat_axis=0, tiled=True)
        flat_returned = returned.reshape(-1, model_width)
        remaining = spread_weight[:, :, window].reshape(length, -1)
        for _ in range(3):
            part = lax.reduce_precision(remaining, exponent_bits=8, mantissa_bits=7)
            total = total + jnp.dot(
                part.astype(jnp.bfloat16), flat_returned, preferred_element_type=jnp.float32
            )
            remaining = remaining - part
    return total.astype(jnp.bfloat16)


def solution(mesh):
    fine = jax.sharding.Mesh(
        mesh.devices.reshape(mesh.shape["dp"], 4, -1, 2),
        ("dp",) + SEQ,
    )
    placed = (
        P(("dp",) + SEQ, None),
        P(("dp",) + SEQ, None),
        P(("dp",) + SEQ, None),
        P(("dp",) + SEQ, None),
        P(("dp",) + SEQ, None),
        P("dp", SEQ),
        P("dp", SEQ),
        P(),
        P(SEQ, None),
        P(SEQ, None, None),
        P(SEQ, None, None),
        P(SEQ, None, None),
    )
    return jax.shard_map(
        shards, mesh=fine, in_specs=placed, out_specs=P(("dp",) + SEQ, None), check_vma=False
    )
```

```python
import jax
import jax.numpy as jnp
from jax import lax
from jax.sharding import PartitionSpec as P

SEQ = ("sy", "sx", "sc")
CHIP_AXES = ("sy", "sx")
CORE_AXIS = "sc"
CHUNKS = 1


def carried_in(state, ending, axis):
    count = lax.axis_size(axis)

    def shifted(part, distance):
        pairs = [(j, j + distance) for j in range(count - distance)]
        return lax.ppermute(part, axis, pairs)

    def combine(earlier, latter):
        return (earlier[0] * jnp.exp(latter[1])[:, None, None] + latter[0], earlier[1] + latter[1])

    heads, rows, width = state.shape

    def pieces(wide):
        parts = []
        for _ in range(3):
            part = lax.reduce_precision(wide, exponent_bits=8, mantissa_bits=7)
            parts.append(part.astype(jnp.bfloat16))
            wide = wide - part
        block = jnp.stack(parts, axis=1)
        return jnp.pad(block, ((0, 0), (0, width - 3)))

    def fetch(pair, distance):
        low, wide = pair
        message = jnp.concatenate(
            [low.astype(jnp.bfloat16).reshape(heads * rows, width), pieces(wide)], axis=0
        )
        arrived = shifted(message, distance)
        body = arrived[: heads * rows].reshape(heads, rows, width).astype(jnp.float32)
        tail = arrived[heads * rows :, :3].astype(jnp.float32)
        return (body, tail[:, 0] + tail[:, 1] + tail[:, 2])

    covered = (state, ending)
    reach = 1
    while 2 * reach < count:
        covered = combine(fetch(covered, reach), covered)
        reach *= 2
    if count == 1:
        return jnp.zeros_like(state)
    near = fetch(covered, 1)
    if reach + 1 < count:
        near = combine(fetch(covered, reach + 1), near)
    return near[0]


def shards(
    queries,
    keys_in,
    values,
    stream,
    log_decay,
    token_index,
    route_weight,
    moe_gain,
    out_weight,
    gate_weight,
    up_weight,
    down_weight,
):
    length, model_width = queries.shape
    head_count = log_decay.shape[1]
    head_size = model_width // head_count
    scaling = head_size ** (-0.5)
    device = lax.axis_index(SEQ)
    query_heads = queries.reshape(length, head_count, head_size).transpose(1, 0, 2)
    key_heads = keys_in.reshape(length, head_count, head_size).transpose(1, 0, 2)
    value_heads = values.reshape(length, head_count, head_size).transpose(1, 0, 2)
    running = jnp.cumsum(log_decay, axis=0).T
    ending = running[:, -1]
    shrink = jnp.exp(ending[:, None] - running)
    key_scaled = (key_heads.astype(jnp.float32) * shrink[:, :, None]).astype(jnp.bfloat16)
    local_state = jnp.einsum(
        "hsd,hse->hde", key_scaled, value_heads, preferred_element_type=jnp.float32
    )
    incoming = carried_in(local_state, ending, SEQ)
    scores = (
        jnp.einsum("htd,hsd->hts", query_heads, key_heads, preferred_element_type=jnp.float32)
        * scaling
    )
    spacing = running[:, :, None] - running[:, None, :]
    causal = jnp.arange(length)[:, None] >= jnp.arange(length)[None, :]
    decay_mask = jnp.where(causal[None], jnp.exp(jnp.minimum(spacing, 0.0)), 0.0)
    attend_weights = (scores * decay_mask).astype(jnp.bfloat16)
    within = jnp.einsum(
        "hts,hsd->htd", attend_weights, value_heads, preferred_element_type=jnp.float32
    )
    query_scaled = (
        query_heads.astype(jnp.float32) * (jnp.exp(running) * scaling)[:, :, None]
    ).astype(jnp.bfloat16)
    within, query_scaled = lax.optimization_barrier((within, query_scaled))
    across = jnp.einsum(
        "htd,hde->hte",
        query_scaled,
        incoming.astype(jnp.bfloat16),
        preferred_element_type=jnp.float32,
    )
    unnormed = within + across
    spread = jnp.mean(unnormed * unnormed, axis=2, keepdims=True)
    normed = (
        (unnormed * lax.rsqrt(spread + 1e-06))
        .astype(jnp.bfloat16)
        .transpose(1, 0, 2)
        .reshape(length, model_width)
    )
    attended = jnp.dot(
        normed,
        lax.all_gather(out_weight, SEQ, axis=0, tiled=True),
        preferred_element_type=jnp.float32,
    )
    residual = (stream.astype(jnp.float32) + attended).astype(jnp.bfloat16)
    widened = residual.astype(jnp.float32)
    mixed_in = (
        widened * lax.rsqrt(jnp.mean(widened * widened, axis=1, keepdims=True) + 1e-06) * moe_gain
    ).astype(jnp.bfloat16)
    offsets = (token_index - device * length).reshape(-1)
    positions = jnp.arange(length)
    choose = (offsets[:, None] == positions[None, :]).astype(jnp.bfloat16)
    picked = jnp.dot(choose, mixed_in, preferred_element_type=jnp.float32).astype(jnp.bfloat16)
    picked = picked.reshape(token_index.shape + (model_width,))
    spread_weight = jnp.where(
        positions[:, None] == offsets[None, :], route_weight.reshape(-1)[None, :], 0.0
    ).reshape((length,) + token_index.shape)
    slots = token_index.shape[1]
    step = slots // CHUNKS
    total = widened
    for chunk in range(CHUNKS):
        window = slice(chunk * step, (chunk + 1) * step)
        arrived = lax.all_to_all(picked[:, window], SEQ, split_axis=0, concat_axis=0, tiled=True)
        gating = jnp.einsum(
            "snd,df->snf", arrived, gate_weight[0], preferred_element_type=jnp.float32
        )
        upward = jnp.einsum("snd,df->snf", arrived, up_weight[0], preferred_element_type=jnp.float32)
        activated = (jax.nn.silu(gating) * upward).astype(jnp.bfloat16)
        produced = jnp.einsum(
            "snf,fd->snd", activated, down_weight[0], preferred_element_type=jnp.float32
        ).astype(jnp.bfloat16)
        returned = lax.all_to_all(produced, SEQ, split_axis=0, concat_axis=0, tiled=True)
        flat_returned = returned.reshape(-1, model_width)
        remaining = spread_weight[:, :, window].reshape(length, -1)
        for _ in range(3):
            part = lax.reduce_precision(remaining, exponent_bits=8, mantissa_bits=7)
            total = total + jnp.dot(
                part.astype(jnp.bfloat16), flat_returned, preferred_element_type=jnp.float32
            )
            remaining = remaining - part
    return total.astype(jnp.bfloat16)


def solution(mesh):
    fine = jax.sharding.Mesh(
        mesh.devices.reshape(mesh.shape["dp"], 4, -1, 2),
        ("dp",) + SEQ,
    )
    placed = (
        P(("dp",) + SEQ, None),
        P(("dp",) + SEQ, None),
        P(("dp",) + SEQ, None),
        P(("dp",) + SEQ, None),
        P(("dp",) + SEQ, None),
        P("dp", SEQ),
        P("dp", SEQ),
        P(),
        P(SEQ, None),
        P(SEQ, None, None),
        P(SEQ, None, None),
        P(SEQ, None, None),
    )
    return jax.shard_map(
        shards, mesh=fine, in_specs=placed, out_specs=P(("dp",) + SEQ, None), check_vma=False
    )
```

```python
import jax
import jax.numpy as jnp
from jax import lax
from jax.sharding import PartitionSpec as P

SEQ = ("sy", "sx", "sc")
CHIP_AXES = ("sy", "sx")
CORE_AXIS = "sc"
CHUNKS = 1
TIE_REACH = 8


def carried_in(state, ending, axis, rider):
    count = lax.axis_size(axis)

    def shifted(part, distance):
        pairs = [(j, j + distance) for j in range(count - distance)]
        return lax.ppermute(part, axis, pairs)

    def combine(earlier, latter):
        return (earlier[0] * jnp.exp(latter[1])[:, None, None] + latter[0], earlier[1] + latter[1])

    heads, rows, width = state.shape

    def pieces(wide):
        parts = []
        for _ in range(3):
            part = lax.reduce_precision(wide, exponent_bits=8, mantissa_bits=7)
            parts.append(part.astype(jnp.bfloat16))
            wide = wide - part
        block = jnp.stack(parts, axis=1)
        return jnp.pad(block, ((0, 0), (0, width - 3)))

    def fetch(pair, distance):
        low, wide = pair
        message = jnp.concatenate(
            [low.astype(jnp.bfloat16).reshape(heads * rows, width), pieces(wide)], axis=0
        )
        arrived = shifted(message, distance)
        body = arrived[: heads * rows].reshape(heads, rows, width).astype(jnp.float32)
        tail = arrived[heads * rows :, :3].astype(jnp.float32)
        return (body, tail[:, 0] + tail[:, 1] + tail[:, 2])

    covered = (state, ending)
    reach = 1
    while 2 * reach < count:
        covered = combine(fetch(covered, reach), covered)
        reach *= 2
        if reach == TIE_REACH:
            covered, rider = lax.optimization_barrier((covered, rider))
    if count == 1:
        return jnp.zeros_like(state)
    near = fetch(covered, 1)
    if reach + 1 < count:
        near = combine(fetch(covered, reach + 1), near)
    return near[0], rider


def shards(
    queries,
    keys_in,
    values,
    stream,
    log_decay,
    token_index,
    route_weight,
    moe_gain,
    out_weight,
    gate_weight,
    up_weight,
    down_weight,
):
    length, model_width = queries.shape
    head_count = log_decay.shape[1]
    head_size = model_width // head_count
    scaling = head_size ** (-0.5)
    device = lax.axis_index(SEQ)
    query_heads = queries.reshape(length, head_count, head_size).transpose(1, 0, 2)
    key_heads = keys_in.reshape(length, head_count, head_size).transpose(1, 0, 2)
    value_heads = values.reshape(length, head_count, head_size).transpose(1, 0, 2)
    running = jnp.cumsum(log_decay, axis=0).T
    ending = running[:, -1]
    shrink = jnp.exp(ending[:, None] - running)
    key_scaled = (key_heads.astype(jnp.float32) * shrink[:, :, None]).astype(jnp.bfloat16)
    local_state = jnp.einsum(
        "hsd,hse->hde", key_scaled, value_heads, preferred_element_type=jnp.float32
    )
    chips = lax.all_gather(out_weight, CHIP_AXES, axis=0, tiled=True)
    incoming, chips = carried_in(local_state, ending, SEQ, chips)
    other = lax.ppermute(chips, CORE_AXIS, [(0, 1), (1, 0)])
    scores = (
        jnp.einsum("htd,hsd->hts", query_heads, key_heads, preferred_element_type=jnp.float32)
        * scaling
    )
    spacing = running[:, :, None] - running[:, None, :]
    causal = jnp.arange(length)[:, None] >= jnp.arange(length)[None, :]
    decay_mask = jnp.where(causal[None], jnp.exp(jnp.minimum(spacing, 0.0)), 0.0)
    attend_weights = (scores * decay_mask).astype(jnp.bfloat16)
    within = jnp.einsum(
        "hts,hsd->htd", attend_weights, value_heads, preferred_element_type=jnp.float32
    )
    query_scaled = (
        query_heads.astype(jnp.float32) * (jnp.exp(running) * scaling)[:, :, None]
    ).astype(jnp.bfloat16)
    within, query_scaled = lax.optimization_barrier((within, query_scaled))
    across = jnp.einsum(
        "htd,hde->hte",
        query_scaled,
        incoming.astype(jnp.bfloat16),
        preferred_element_type=jnp.float32,
    )
    unnormed = within + across
    spread = jnp.mean(unnormed * unnormed, axis=2, keepdims=True)
    normed = (
        (unnormed * lax.rsqrt(spread + 1e-06))
        .astype(jnp.bfloat16)
        .transpose(1, 0, 2)
        .reshape(length, model_width)
    )
    core = lax.axis_index(CORE_AXIS)
    split = normed.reshape(length, -1, 2, out_weight.shape[0])
    shaped = (-1, out_weight.shape[0], model_width)
    attended = jnp.einsum(
        "tbr,brd->td",
        lax.dynamic_index_in_dim(split, core, axis=2, keepdims=False),
        chips.reshape(shaped),
        preferred_element_type=jnp.float32,
    ) + jnp.einsum(
        "tbr,brd->td",
        lax.dynamic_index_in_dim(split, 1 - core, axis=2, keepdims=False),
        other.reshape(shaped),
        preferred_element_type=jnp.float32,
    )
    residual = (stream.astype(jnp.float32) + attended).astype(jnp.bfloat16)
    widened = residual.astype(jnp.float32)
    mixed_in = (
        widened * lax.rsqrt(jnp.mean(widened * widened, axis=1, keepdims=True) + 1e-06) * moe_gain
    ).astype(jnp.bfloat16)
    offsets = (token_index - device * length).reshape(-1)
    positions = jnp.arange(length)
    choose = (offsets[:, None] == positions[None, :]).astype(jnp.bfloat16)
    picked = jnp.dot(choose, mixed_in, preferred_element_type=jnp.float32).astype(jnp.bfloat16)
    picked = picked.reshape(token_index.shape + (model_width,))
    spread_weight = jnp.where(
        positions[:, None] == offsets[None, :], route_weight.reshape(-1)[None, :], 0.0
    ).reshape((length,) + token_index.shape)
    slots = token_index.shape[1]
    step = slots // CHUNKS
    total = widened
    for chunk in range(CHUNKS):
        window = slice(chunk * step, (chunk + 1) * step)
        arrived = lax.all_to_all(picked[:, window], SEQ, split_axis=0, concat_axis=0, tiled=True)
        gating = jnp.einsum(
            "snd,df->snf", arrived, gate_weight[0], preferred_element_type=jnp.float32
        )
        upward = jnp.einsum("snd,df->snf", arrived, up_weight[0], preferred_element_type=jnp.float32)
        activated = (jax.nn.silu(gating) * upward).astype(jnp.bfloat16)
        produced = jnp.einsum(
            "snf,fd->snd", activated, down_weight[0], preferred_element_type=jnp.float32
        ).astype(jnp.bfloat16)
        returned = lax.all_to_all(produced, SEQ, split_axis=0, concat_axis=0, tiled=True)
        flat_returned = returned.reshape(-1, model_width)
        remaining = spread_weight[:, :, window].reshape(length, -1)
        for _ in range(2):
            part = lax.reduce_precision(remaining, exponent_bits=8, mantissa_bits=7)
            total = total + jnp.dot(
                part.astype(jnp.bfloat16), flat_returned, preferred_element_type=jnp.float32
            )
            remaining = remaining - part
    return total.astype(jnp.bfloat16)


def solution(mesh):
    fine = jax.sharding.Mesh(
        mesh.devices.reshape(mesh.shape["dp"], 4, -1, 2),
        ("dp",) + SEQ,
    )
    placed = (
        P(("dp",) + SEQ, None),
        P(("dp",) + SEQ, None),
        P(("dp",) + SEQ, None),
        P(("dp",) + SEQ, None),
        P(("dp",) + SEQ, None),
        P("dp", SEQ),
        P("dp", SEQ),
        P(),
        P(SEQ, None),
        P(SEQ, None, None),
        P(SEQ, None, None),
        P(SEQ, None, None),
    )
    return jax.shard_map(
        shards, mesh=fine, in_specs=placed, out_specs=P(("dp",) + SEQ, None), check_vma=False
    )
```

```python
import jax
import jax.numpy as jnp
from jax import lax
from jax.sharding import PartitionSpec as P

SEQ = ("sy", "sx", "sc")
CHIP_AXES = ("sy", "sx")
CORE_AXIS = "sc"
CHUNKS = 1


def pack(state, ending):
    heads, rows, width = state.shape
    wide, parts = ending, []
    for _ in range(3):
        part = lax.reduce_precision(wide, exponent_bits=8, mantissa_bits=7)
        parts.append(part.astype(jnp.bfloat16))
        wide = wide - part
    block = jnp.pad(jnp.stack(parts, axis=1), ((0, 0), (0, width - 3)))
    return jnp.concatenate(
        [state.astype(jnp.bfloat16).reshape(heads * rows, width), block], axis=0
    )


def unpack(message, heads):
    width = message.shape[1]
    body = message[: heads * width].reshape(heads, width, width).astype(jnp.float32)
    tail = message[heads * width :, :3].astype(jnp.float32)
    return body, tail[:, 0] + tail[:, 1] + tail[:, 2]


def combine(earlier, latter):
    return (earlier[0] * jnp.exp(latter[1])[:, None, None] + latter[0], earlier[1] + latter[1])


def exclusive_scan(state, ending, axis):
    count = lax.axis_size(axis)
    heads = state.shape[0]

    def fetch(pair, distance):
        pairs = [(j, j + distance) for j in range(count - distance)]
        return unpack(lax.ppermute(pack(*pair), axis, pairs), heads)

    covered = (state, ending)
    reach = 1
    while 2 * reach < count:
        covered = combine(fetch(covered, reach), covered)
        reach *= 2
    if count == 1:
        return jnp.zeros_like(state)
    near = fetch(covered, 1)
    if reach + 1 < count:
        near = combine(fetch(covered, reach + 1), near)
    return near[0]


def carried_in(state, ending):
    heads = state.shape[0]
    half = heads // 2
    swap = [(0, 1), (1, 0)]
    core = lax.axis_index(CORE_AXIS)
    first = core == 0
    other_state, other_ending = unpack(lax.ppermute(pack(state, ending), CORE_AXIS, swap), heads)
    lower = (jnp.where(first, state, other_state), jnp.where(first, ending, other_ending))
    upper = (jnp.where(first, other_state, state), jnp.where(first, other_ending, ending))
    chip_state, chip_ending = combine(lower, upper)
    mine = exclusive_scan(
        lax.dynamic_slice_in_dim(chip_state, core * half, half, axis=0),
        lax.dynamic_slice_in_dim(chip_ending, core * half, half, axis=0),
        CHIP_AXES,
    )
    theirs = lax.ppermute(mine.astype(jnp.bfloat16), CORE_AXIS, swap).astype(jnp.float32)
    before = jnp.where(
        first, jnp.concatenate([mine, theirs], axis=0), jnp.concatenate([theirs, mine], axis=0)
    )
    return jnp.where(first, before, combine((before, 0.0), lower)[0])


def shards(
    queries,
    keys_in,
    values,
    stream,
    log_decay,
    token_index,
    route_weight,
    moe_gain,
    out_weight,
    gate_weight,
    up_weight,
    down_weight,
):
    length, model_width = queries.shape
    head_count = log_decay.shape[1]
    head_size = model_width // head_count
    scaling = head_size ** (-0.5)
    device = lax.axis_index(SEQ)
    query_heads = queries.reshape(length, head_count, head_size).transpose(1, 0, 2)
    key_heads = keys_in.reshape(length, head_count, head_size).transpose(1, 0, 2)
    value_heads = values.reshape(length, head_count, head_size).transpose(1, 0, 2)
    running = jnp.cumsum(log_decay, axis=0).T
    ending = running[:, -1]
    shrink = jnp.exp(ending[:, None] - running)
    key_scaled = (key_heads.astype(jnp.float32) * shrink[:, :, None]).astype(jnp.bfloat16)
    local_state = jnp.einsum(
        "hsd,hse->hde", key_scaled, value_heads, preferred_element_type=jnp.float32
    )
    incoming = carried_in(local_state, ending)
    scores = (
        jnp.einsum("htd,hsd->hts", query_heads, key_heads, preferred_element_type=jnp.float32)
        * scaling
    )
    spacing = running[:, :, None] - running[:, None, :]
    causal = jnp.arange(length)[:, None] >= jnp.arange(length)[None, :]
    decay_mask = jnp.where(causal[None], jnp.exp(jnp.minimum(spacing, 0.0)), 0.0)
    attend_weights = (scores * decay_mask).astype(jnp.bfloat16)
    within = jnp.einsum(
        "hts,hsd->htd", attend_weights, value_heads, preferred_element_type=jnp.float32
    )
    query_scaled = (
        query_heads.astype(jnp.float32) * (jnp.exp(running) * scaling)[:, :, None]
    ).astype(jnp.bfloat16)
    within, query_scaled = lax.optimization_barrier((within, query_scaled))
    across = jnp.einsum(
        "htd,hde->hte",
        query_scaled,
        incoming.astype(jnp.bfloat16),
        preferred_element_type=jnp.float32,
    )
    unnormed = within + across
    spread = jnp.mean(unnormed * unnormed, axis=2, keepdims=True)
    normed = (
        (unnormed * lax.rsqrt(spread + 1e-06))
        .astype(jnp.bfloat16)
        .transpose(1, 0, 2)
        .reshape(length, model_width)
    )
    attended = jnp.dot(
        normed,
        lax.all_gather(out_weight, SEQ, axis=0, tiled=True),
        preferred_element_type=jnp.float32,
    )
    residual = (stream.astype(jnp.float32) + attended).astype(jnp.bfloat16)
    widened = residual.astype(jnp.float32)
    mixed_in = (
        widened * lax.rsqrt(jnp.mean(widened * widened, axis=1, keepdims=True) + 1e-06) * moe_gain
    ).astype(jnp.bfloat16)
    offsets = (token_index - device * length).reshape(-1)
    positions = jnp.arange(length)
    choose = (offsets[:, None] == positions[None, :]).astype(jnp.bfloat16)
    picked = jnp.dot(choose, mixed_in, preferred_element_type=jnp.float32).astype(jnp.bfloat16)
    picked = picked.reshape(token_index.shape + (model_width,))
    spread_weight = jnp.where(
        positions[:, None] == offsets[None, :], route_weight.reshape(-1)[None, :], 0.0
    ).reshape((length,) + token_index.shape)
    slots = token_index.shape[1]
    step = slots // CHUNKS
    total = widened
    for chunk in range(CHUNKS):
        window = slice(chunk * step, (chunk + 1) * step)
        arrived = lax.all_to_all(picked[:, window], SEQ, split_axis=0, concat_axis=0, tiled=True)
        gating = jnp.einsum(
            "snd,df->snf", arrived, gate_weight[0], preferred_element_type=jnp.float32
        )
        upward = jnp.einsum("snd,df->snf", arrived, up_weight[0], preferred_element_type=jnp.float32)
        activated = (jax.nn.silu(gating) * upward).astype(jnp.bfloat16)
        produced = jnp.einsum(
            "snf,fd->snd", activated, down_weight[0], preferred_element_type=jnp.float32
        ).astype(jnp.bfloat16)
        returned = lax.all_to_all(produced, SEQ, split_axis=0, concat_axis=0, tiled=True)
        flat_returned = returned.reshape(-1, model_width)
        remaining = spread_weight[:, :, window].reshape(length, -1)
        for _ in range(2):
            part = lax.reduce_precision(remaining, exponent_bits=8, mantissa_bits=7)
            total = total + jnp.dot(
                part.astype(jnp.bfloat16), flat_returned, preferred_element_type=jnp.float32
            )
            remaining = remaining - part
    return total.astype(jnp.bfloat16)


def solution(mesh):
    fine = jax.sharding.Mesh(
        mesh.devices.reshape(mesh.shape["dp"], 4, -1, 2),
        ("dp",) + SEQ,
    )
    placed = (
        P(("dp",) + SEQ, None),
        P(("dp",) + SEQ, None),
        P(("dp",) + SEQ, None),
        P(("dp",) + SEQ, None),
        P(("dp",) + SEQ, None),
        P("dp", SEQ),
        P("dp", SEQ),
        P(),
        P(SEQ, None),
        P(SEQ, None, None),
        P(SEQ, None, None),
        P(SEQ, None, None),
    )
    return jax.shard_map(
        shards, mesh=fine, in_specs=placed, out_specs=P(("dp",) + SEQ, None), check_vma=False
    )
```

```python
import jax
import jax.numpy as jnp
from jax import lax
from jax.sharding import PartitionSpec as P

SEQ = ("sy", "sx", "sc")
CHIP_AXES = ("sy", "sx")
CORE_AXIS = "sc"
CHUNKS = 1
RADIX = 4


def pack(state, ending):
    heads, rows, width = state.shape
    wide, parts = ending, []
    for _ in range(3):
        part = lax.reduce_precision(wide, exponent_bits=8, mantissa_bits=7)
        parts.append(part.astype(jnp.bfloat16))
        wide = wide - part
    block = jnp.pad(jnp.stack(parts, axis=1), ((0, 0), (0, width - 3)))
    return jnp.concatenate(
        [state.astype(jnp.bfloat16).reshape(heads * rows, width), block], axis=0
    )


def unpack(message, heads):
    width = message.shape[1]
    body = message[: heads * width].reshape(heads, width, width).astype(jnp.float32)
    tail = message[heads * width :, :3].astype(jnp.float32)
    return body, tail[:, 0] + tail[:, 1] + tail[:, 2]


def combine(earlier, latter):
    return (earlier[0] * jnp.exp(latter[1])[:, None, None] + latter[0], earlier[1] + latter[1])


def exclusive_scan(state, ending, axis):
    count = lax.axis_size(axis)
    heads = state.shape[0]

    def fetch(pair, distance):
        pairs = [(j, j + distance) for j in range(count - distance)]
        return unpack(lax.ppermute(pack(*pair), axis, pairs), heads)

    covered = (state, ending)
    reach = 1
    while reach * RADIX < count:
        gathered = covered
        for multiple in range(1, RADIX):
            gathered = combine(fetch(covered, multiple * reach), gathered)
        covered = gathered
        reach *= RADIX
    if count == 1:
        return jnp.zeros_like(state)
    near = fetch(covered, 1)
    distance = 1 + reach
    while distance < count:
        near = combine(fetch(covered, distance), near)
        distance += reach
    return near[0]


def carried_in(state, ending):
    heads = state.shape[0]
    half = heads // 2
    swap = [(0, 1), (1, 0)]
    core = lax.axis_index(CORE_AXIS)
    first = core == 0
    other_state, other_ending = unpack(lax.ppermute(pack(state, ending), CORE_AXIS, swap), heads)
    lower = (jnp.where(first, state, other_state), jnp.where(first, ending, other_ending))
    upper = (jnp.where(first, other_state, state), jnp.where(first, other_ending, ending))
    chip_state, chip_ending = combine(lower, upper)
    mine = exclusive_scan(
        lax.dynamic_slice_in_dim(chip_state, core * half, half, axis=0),
        lax.dynamic_slice_in_dim(chip_ending, core * half, half, axis=0),
        CHIP_AXES,
    )
    theirs = lax.ppermute(mine.astype(jnp.bfloat16), CORE_AXIS, swap).astype(jnp.float32)
    before = jnp.where(
        first, jnp.concatenate([mine, theirs], axis=0), jnp.concatenate([theirs, mine], axis=0)
    )
    return jnp.where(first, before, combine((before, 0.0), lower)[0])


def shards(
    queries,
    keys_in,
    values,
    stream,
    log_decay,
    token_index,
    route_weight,
    moe_gain,
    out_weight,
    gate_weight,
    up_weight,
    down_weight,
):
    length, model_width = queries.shape
    head_count = log_decay.shape[1]
    head_size = model_width // head_count
    scaling = head_size ** (-0.5)
    device = lax.axis_index(SEQ)
    query_heads = queries.reshape(length, head_count, head_size).transpose(1, 0, 2)
    key_heads = keys_in.reshape(length, head_count, head_size).transpose(1, 0, 2)
    value_heads = values.reshape(length, head_count, head_size).transpose(1, 0, 2)
    running = jnp.cumsum(log_decay, axis=0).T
    ending = running[:, -1]
    shrink = jnp.exp(ending[:, None] - running)
    key_scaled = (key_heads.astype(jnp.float32) * shrink[:, :, None]).astype(jnp.bfloat16)
    local_state = jnp.einsum(
        "hsd,hse->hde", key_scaled, value_heads, preferred_element_type=jnp.float32
    )
    incoming = carried_in(local_state, ending)
    scores = (
        jnp.einsum("htd,hsd->hts", query_heads, key_heads, preferred_element_type=jnp.float32)
        * scaling
    )
    spacing = running[:, :, None] - running[:, None, :]
    causal = jnp.arange(length)[:, None] >= jnp.arange(length)[None, :]
    decay_mask = jnp.where(causal[None], jnp.exp(jnp.minimum(spacing, 0.0)), 0.0)
    attend_weights = (scores * decay_mask).astype(jnp.bfloat16)
    within = jnp.einsum(
        "hts,hsd->htd", attend_weights, value_heads, preferred_element_type=jnp.float32
    )
    query_scaled = (
        query_heads.astype(jnp.float32) * (jnp.exp(running) * scaling)[:, :, None]
    ).astype(jnp.bfloat16)
    within, query_scaled = lax.optimization_barrier((within, query_scaled))
    across = jnp.einsum(
        "htd,hde->hte",
        query_scaled,
        incoming.astype(jnp.bfloat16),
        preferred_element_type=jnp.float32,
    )
    unnormed = within + across
    spread = jnp.mean(unnormed * unnormed, axis=2, keepdims=True)
    normed = (
        (unnormed * lax.rsqrt(spread + 1e-06))
        .astype(jnp.bfloat16)
        .transpose(1, 0, 2)
        .reshape(length, model_width)
    )
    attended = jnp.dot(
        normed,
        lax.all_gather(out_weight, SEQ, axis=0, tiled=True),
        preferred_element_type=jnp.float32,
    )
    residual = (stream.astype(jnp.float32) + attended).astype(jnp.bfloat16)
    widened = residual.astype(jnp.float32)
    mixed_in = (
        widened * lax.rsqrt(jnp.mean(widened * widened, axis=1, keepdims=True) + 1e-06) * moe_gain
    ).astype(jnp.bfloat16)
    offsets = (token_index - device * length).reshape(-1)
    positions = jnp.arange(length)
    choose = (offsets[:, None] == positions[None, :]).astype(jnp.bfloat16)
    picked = jnp.dot(choose, mixed_in, preferred_element_type=jnp.float32).astype(jnp.bfloat16)
    picked = picked.reshape(token_index.shape + (model_width,))
    spread_weight = jnp.where(
        positions[:, None] == offsets[None, :], route_weight.reshape(-1)[None, :], 0.0
    ).reshape((length,) + token_index.shape)
    slots = token_index.shape[1]
    step = slots // CHUNKS
    total = widened
    for chunk in range(CHUNKS):
        window = slice(chunk * step, (chunk + 1) * step)
        arrived = lax.all_to_all(picked[:, window], SEQ, split_axis=0, concat_axis=0, tiled=True)
        gating = jnp.einsum(
            "snd,df->snf", arrived, gate_weight[0], preferred_element_type=jnp.float32
        )
        upward = jnp.einsum("snd,df->snf", arrived, up_weight[0], preferred_element_type=jnp.float32)
        activated = (jax.nn.silu(gating) * upward).astype(jnp.bfloat16)
        produced = jnp.einsum(
            "snf,fd->snd", activated, down_weight[0], preferred_element_type=jnp.float32
        ).astype(jnp.bfloat16)
        returned = lax.all_to_all(produced, SEQ, split_axis=0, concat_axis=0, tiled=True)
        flat_returned = returned.reshape(-1, model_width)
        remaining = spread_weight[:, :, window].reshape(length, -1)
        for _ in range(2):
            part = lax.reduce_precision(remaining, exponent_bits=8, mantissa_bits=7)
            total = total + jnp.dot(
                part.astype(jnp.bfloat16), flat_returned, preferred_element_type=jnp.float32
            )
            remaining = remaining - part
    return total.astype(jnp.bfloat16)


def solution(mesh):
    fine = jax.sharding.Mesh(
        mesh.devices.reshape(mesh.shape["dp"], 4, -1, 2),
        ("dp",) + SEQ,
    )
    placed = (
        P(("dp",) + SEQ, None),
        P(("dp",) + SEQ, None),
        P(("dp",) + SEQ, None),
        P(("dp",) + SEQ, None),
        P(("dp",) + SEQ, None),
        P("dp", SEQ),
        P("dp", SEQ),
        P(),
        P(SEQ, None),
        P(SEQ, None, None),
        P(SEQ, None, None),
        P(SEQ, None, None),
    )
    return jax.shard_map(
        shards, mesh=fine, in_specs=placed, out_specs=P(("dp",) + SEQ, None), check_vma=False
    )
```

```python
import jax
import jax.numpy as jnp
from jax import lax
from jax.sharding import PartitionSpec as P

SEQ = ("sy", "sx", "sc")
CHIP_AXES = ("sy", "sx")
CORE_AXIS = "sc"
CHUNKS = 1


def pack(state, ending):
    heads, rows, width = state.shape
    wide, parts = ending, []
    for _ in range(3):
        part = lax.reduce_precision(wide, exponent_bits=8, mantissa_bits=7)
        parts.append(part.astype(jnp.bfloat16))
        wide = wide - part
    block = jnp.pad(jnp.stack(parts, axis=1), ((0, 0), (0, width - 3)))
    return jnp.concatenate(
        [state.astype(jnp.bfloat16).reshape(heads * rows, width), block], axis=0
    )


def unpack(message, heads):
    width = message.shape[1]
    body = message[: heads * width].reshape(heads, width, width).astype(jnp.float32)
    tail = message[heads * width :, :3].astype(jnp.float32)
    return body, tail[:, 0] + tail[:, 1] + tail[:, 2]


def combine(earlier, latter):
    return (earlier[0] * jnp.exp(latter[1])[:, None, None] + latter[0], earlier[1] + latter[1])


def exclusive_scan(state, ending, axis, rider):
    count = lax.axis_size(axis)
    heads = state.shape[0]

    def fetch(pair, distance):
        pairs = [(j, j + distance) for j in range(count - distance)]
        return unpack(lax.ppermute(pack(*pair), axis, pairs), heads)

    covered = (state, ending)
    reach = 1
    while 2 * reach < count:
        covered = combine(fetch(covered, reach), covered)
        if reach == 1:
            covered, rider = lax.optimization_barrier((covered, rider))
        reach *= 2
    if count == 1:
        return jnp.zeros_like(state), rider
    near = fetch(covered, 1)
    if reach + 1 < count:
        near = combine(fetch(covered, reach + 1), near)
    return near[0], rider


def carried_in(state, ending, rider):
    heads = state.shape[0]
    half = heads // 2
    swap = [(0, 1), (1, 0)]
    core = lax.axis_index(CORE_AXIS)
    first = core == 0
    other_state, other_ending = unpack(lax.ppermute(pack(state, ending), CORE_AXIS, swap), heads)
    lower = (jnp.where(first, state, other_state), jnp.where(first, ending, other_ending))
    upper = (jnp.where(first, other_state, state), jnp.where(first, other_ending, ending))
    chip_state, chip_ending = combine(lower, upper)
    mine, rider = exclusive_scan(
        lax.dynamic_slice_in_dim(chip_state, core * half, half, axis=0),
        lax.dynamic_slice_in_dim(chip_ending, core * half, half, axis=0),
        CHIP_AXES,
        rider,
    )
    theirs = lax.ppermute(mine.astype(jnp.bfloat16), CORE_AXIS, swap).astype(jnp.float32)
    before = jnp.where(
        first, jnp.concatenate([mine, theirs], axis=0), jnp.concatenate([theirs, mine], axis=0)
    )
    return jnp.where(first, before, combine((before, 0.0), lower)[0]), rider


def shards(
    queries,
    keys_in,
    values,
    stream,
    log_decay,
    token_index,
    route_weight,
    moe_gain,
    out_weight,
    gate_weight,
    up_weight,
    down_weight,
):
    length, model_width = queries.shape
    head_count = log_decay.shape[1]
    head_size = model_width // head_count
    scaling = head_size ** (-0.5)
    device = lax.axis_index(SEQ)
    query_heads = queries.reshape(length, head_count, head_size).transpose(1, 0, 2)
    key_heads = keys_in.reshape(length, head_count, head_size).transpose(1, 0, 2)
    value_heads = values.reshape(length, head_count, head_size).transpose(1, 0, 2)
    running = jnp.cumsum(log_decay, axis=0).T
    ending = running[:, -1]
    shrink = jnp.exp(ending[:, None] - running)
    key_scaled = (key_heads.astype(jnp.float32) * shrink[:, :, None]).astype(jnp.bfloat16)
    local_state = jnp.einsum(
        "hsd,hse->hde", key_scaled, value_heads, preferred_element_type=jnp.float32
    )
    incoming, out_weight = carried_in(local_state, ending, out_weight)
    scores = (
        jnp.einsum("htd,hsd->hts", query_heads, key_heads, preferred_element_type=jnp.float32)
        * scaling
    )
    spacing = running[:, :, None] - running[:, None, :]
    causal = jnp.arange(length)[:, None] >= jnp.arange(length)[None, :]
    decay_mask = jnp.where(causal[None], jnp.exp(jnp.minimum(spacing, 0.0)), 0.0)
    attend_weights = (scores * decay_mask).astype(jnp.bfloat16)
    within = jnp.einsum(
        "hts,hsd->htd", attend_weights, value_heads, preferred_element_type=jnp.float32
    )
    query_scaled = (
        query_heads.astype(jnp.float32) * (jnp.exp(running) * scaling)[:, :, None]
    ).astype(jnp.bfloat16)
    within, query_scaled = lax.optimization_barrier((within, query_scaled))
    across = jnp.einsum(
        "htd,hde->hte",
        query_scaled,
        incoming.astype(jnp.bfloat16),
        preferred_element_type=jnp.float32,
    )
    unnormed = within + across
    spread = jnp.mean(unnormed * unnormed, axis=2, keepdims=True)
    normed = (
        (unnormed * lax.rsqrt(spread + 1e-06))
        .astype(jnp.bfloat16)
        .transpose(1, 0, 2)
        .reshape(length, model_width)
    )
    attended = jnp.dot(
        normed,
        lax.all_gather(out_weight, SEQ, axis=0, tiled=True),
        preferred_element_type=jnp.float32,
    )
    residual = (stream.astype(jnp.float32) + attended).astype(jnp.bfloat16)
    widened = residual.astype(jnp.float32)
    mixed_in = (
        widened * lax.rsqrt(jnp.mean(widened * widened, axis=1, keepdims=True) + 1e-06) * moe_gain
    ).astype(jnp.bfloat16)
    offsets = (token_index - device * length).reshape(-1)
    positions = jnp.arange(length)
    choose = (offsets[:, None] == positions[None, :]).astype(jnp.bfloat16)
    picked = jnp.dot(choose, mixed_in, preferred_element_type=jnp.float32).astype(jnp.bfloat16)
    picked = picked.reshape(token_index.shape + (model_width,))
    spread_weight = jnp.where(
        positions[:, None] == offsets[None, :], route_weight.reshape(-1)[None, :], 0.0
    ).reshape((length,) + token_index.shape)
    slots = token_index.shape[1]
    step = slots // CHUNKS
    total = widened
    for chunk in range(CHUNKS):
        window = slice(chunk * step, (chunk + 1) * step)
        arrived = lax.all_to_all(picked[:, window], SEQ, split_axis=0, concat_axis=0, tiled=True)
        gating = jnp.einsum(
            "snd,df->snf", arrived, gate_weight[0], preferred_element_type=jnp.float32
        )
        upward = jnp.einsum("snd,df->snf", arrived, up_weight[0], preferred_element_type=jnp.float32)
        activated = (jax.nn.silu(gating) * upward).astype(jnp.bfloat16)
        produced = jnp.einsum(
            "snf,fd->snd", activated, down_weight[0], preferred_element_type=jnp.float32
        ).astype(jnp.bfloat16)
        returned = lax.all_to_all(produced, SEQ, split_axis=0, concat_axis=0, tiled=True)
        flat_returned = returned.reshape(-1, model_width)
        remaining = spread_weight[:, :, window].reshape(length, -1)
        for _ in range(2):
            part = lax.reduce_precision(remaining, exponent_bits=8, mantissa_bits=7)
            total = total + jnp.dot(
                part.astype(jnp.bfloat16), flat_returned, preferred_element_type=jnp.float32
            )
            remaining = remaining - part
    return total.astype(jnp.bfloat16)


def solution(mesh):
    fine = jax.sharding.Mesh(
        mesh.devices.reshape(mesh.shape["dp"], 4, -1, 2),
        ("dp",) + SEQ,
    )
    placed = (
        P(("dp",) + SEQ, None),
        P(("dp",) + SEQ, None),
        P(("dp",) + SEQ, None),
        P(("dp",) + SEQ, None),
        P(("dp",) + SEQ, None),
        P("dp", SEQ),
        P("dp", SEQ),
        P(),
        P(SEQ, None),
        P(SEQ, None, None),
        P(SEQ, None, None),
        P(SEQ, None, None),
    )
    return jax.shard_map(
        shards, mesh=fine, in_specs=placed, out_specs=P(("dp",) + SEQ, None), check_vma=False
    )
```

```python
import jax
import jax.numpy as jnp
from jax import lax
from jax.sharding import PartitionSpec as P

SEQ = ("sy", "sx", "sc")
CHIP_AXES = ("sy", "sx")
CORE_AXIS = "sc"
CHUNKS = 1
SCATTER_PIECES = 1


def pack(state, ending):
    heads, rows, width = state.shape
    wide, parts = ending, []
    for _ in range(3):
        part = lax.reduce_precision(wide, exponent_bits=8, mantissa_bits=7)
        parts.append(part.astype(jnp.bfloat16))
        wide = wide - part
    block = jnp.pad(jnp.stack(parts, axis=1), ((0, 0), (0, width - 3)))
    return jnp.concatenate(
        [state.astype(jnp.bfloat16).reshape(heads * rows, width), block], axis=0
    )


def unpack(message, heads):
    width = message.shape[1]
    body = message[: heads * width].reshape(heads, width, width).astype(jnp.float32)
    tail = message[heads * width :, :3].astype(jnp.float32)
    return body, tail[:, 0] + tail[:, 1] + tail[:, 2]


def combine(earlier, latter):
    return (earlier[0] * jnp.exp(latter[1])[:, None, None] + latter[0], earlier[1] + latter[1])


def exclusive_scan(state, ending, axis, rider):
    count = lax.axis_size(axis)
    heads = state.shape[0]

    def fetch(pair, distance):
        pairs = [(j, j + distance) for j in range(count - distance)]
        return unpack(lax.ppermute(pack(*pair), axis, pairs), heads)

    covered = (state, ending)
    reach = 1
    while 2 * reach < count:
        covered = combine(fetch(covered, reach), covered)
        if reach == 1:
            covered, rider = lax.optimization_barrier((covered, rider))
        reach *= 2
    if count == 1:
        return jnp.zeros_like(state), rider
    near = fetch(covered, 1)
    if reach + 1 < count:
        near = combine(fetch(covered, reach + 1), near)
    return near[0], rider


def carried_in(state, ending, rider):
    heads = state.shape[0]
    half = heads // 2
    swap = [(0, 1), (1, 0)]
    core = lax.axis_index(CORE_AXIS)
    first = core == 0
    other_state, other_ending = unpack(lax.ppermute(pack(state, ending), CORE_AXIS, swap), heads)
    lower = (jnp.where(first, state, other_state), jnp.where(first, ending, other_ending))
    upper = (jnp.where(first, other_state, state), jnp.where(first, other_ending, ending))
    chip_state, chip_ending = combine(lower, upper)
    mine, rider = exclusive_scan(
        lax.dynamic_slice_in_dim(chip_state, core * half, half, axis=0),
        lax.dynamic_slice_in_dim(chip_ending, core * half, half, axis=0),
        CHIP_AXES,
        rider,
    )
    theirs = lax.ppermute(mine.astype(jnp.bfloat16), CORE_AXIS, swap).astype(jnp.float32)
    before = jnp.where(
        first, jnp.concatenate([mine, theirs], axis=0), jnp.concatenate([theirs, mine], axis=0)
    )
    return jnp.where(first, before, combine((before, 0.0), lower)[0]), rider


def shards(
    queries,
    keys_in,
    values,
    stream,
    log_decay,
    token_index,
    route_weight,
    moe_gain,
    out_weight,
    gate_weight,
    up_weight,
    down_weight,
):
    length, model_width = queries.shape
    head_count = log_decay.shape[1]
    head_size = model_width // head_count
    scaling = head_size ** (-0.5)
    device = lax.axis_index(SEQ)
    query_heads = queries.reshape(length, head_count, head_size).transpose(1, 0, 2)
    key_heads = keys_in.reshape(length, head_count, head_size).transpose(1, 0, 2)
    value_heads = values.reshape(length, head_count, head_size).transpose(1, 0, 2)
    running = jnp.cumsum(log_decay, axis=0).T
    ending = running[:, -1]
    shrink = jnp.exp(ending[:, None] - running)
    key_scaled = (key_heads.astype(jnp.float32) * shrink[:, :, None]).astype(jnp.bfloat16)
    local_state = jnp.einsum(
        "hsd,hse->hde", key_scaled, value_heads, preferred_element_type=jnp.float32
    )
    incoming, out_weight = carried_in(local_state, ending, out_weight)
    scores = (
        jnp.einsum("htd,hsd->hts", query_heads, key_heads, preferred_element_type=jnp.float32)
        * scaling
    )
    spacing = running[:, :, None] - running[:, None, :]
    causal = jnp.arange(length)[:, None] >= jnp.arange(length)[None, :]
    decay_mask = jnp.where(causal[None], jnp.exp(jnp.minimum(spacing, 0.0)), 0.0)
    attend_weights = (scores * decay_mask).astype(jnp.bfloat16)
    within = jnp.einsum(
        "hts,hsd->htd", attend_weights, value_heads, preferred_element_type=jnp.float32
    )
    query_scaled = (
        query_heads.astype(jnp.float32) * (jnp.exp(running) * scaling)[:, :, None]
    ).astype(jnp.bfloat16)
    within, query_scaled = lax.optimization_barrier((within, query_scaled))
    across = jnp.einsum(
        "htd,hde->hte",
        query_scaled,
        incoming.astype(jnp.bfloat16),
        preferred_element_type=jnp.float32,
    )
    unnormed = within + across
    spread = jnp.mean(unnormed * unnormed, axis=2, keepdims=True)
    normed = (
        (unnormed * lax.rsqrt(spread + 1e-06))
        .astype(jnp.bfloat16)
        .transpose(1, 0, 2)
        .reshape(length, model_width)
    )
    attended = jnp.dot(
        normed,
        lax.all_gather(out_weight, SEQ, axis=0, tiled=True),
        preferred_element_type=jnp.float32,
    )
    residual = (stream.astype(jnp.float32) + attended).astype(jnp.bfloat16)
    widened = residual.astype(jnp.float32)
    mixed_in = (
        widened * lax.rsqrt(jnp.mean(widened * widened, axis=1, keepdims=True) + 1e-06) * moe_gain
    ).astype(jnp.bfloat16)
    offsets = (token_index - device * length).reshape(-1)
    positions = jnp.arange(length)
    choose = (offsets[:, None] == positions[None, :]).astype(jnp.bfloat16)
    picked = jnp.dot(choose, mixed_in, preferred_element_type=jnp.float32).astype(jnp.bfloat16)
    picked = picked.reshape(token_index.shape + (model_width,))
    spread_weight = jnp.where(
        positions[:, None] == offsets[None, :], route_weight.reshape(-1)[None, :], 0.0
    ).reshape((length,) + token_index.shape)
    slots = token_index.shape[1]
    step = slots // CHUNKS
    total = widened
    for chunk in range(CHUNKS):
        window = slice(chunk * step, (chunk + 1) * step)
        arrived = lax.all_to_all(picked[:, window], SEQ, split_axis=0, concat_axis=0, tiled=True)
        gating = jnp.einsum(
            "snd,df->snf", arrived, gate_weight[0], preferred_element_type=jnp.float32
        )
        upward = jnp.einsum("snd,df->snf", arrived, up_weight[0], preferred_element_type=jnp.float32)
        activated = (jax.nn.silu(gating) * upward).astype(jnp.bfloat16)
        produced = jnp.einsum(
            "snf,fd->snd", activated, down_weight[0], preferred_element_type=jnp.float32
        ).astype(jnp.bfloat16)
        returned = lax.all_to_all(produced, SEQ, split_axis=0, concat_axis=0, tiled=True)
        flat_returned = returned.reshape(-1, model_width)
        remaining = spread_weight[:, :, window].reshape(length, -1)
        for _ in range(SCATTER_PIECES):
            part = lax.reduce_precision(remaining, exponent_bits=8, mantissa_bits=7)
            total = total + jnp.dot(
                part.astype(jnp.bfloat16), flat_returned, preferred_element_type=jnp.float32
            )
            remaining = remaining - part
    return total.astype(jnp.bfloat16)


def solution(mesh):
    fine = jax.sharding.Mesh(
        mesh.devices.reshape(mesh.shape["dp"], 4, -1, 2),
        ("dp",) + SEQ,
    )
    placed = (
        P(("dp",) + SEQ, None),
        P(("dp",) + SEQ, None),
        P(("dp",) + SEQ, None),
        P(("dp",) + SEQ, None),
        P(("dp",) + SEQ, None),
        P("dp", SEQ),
        P("dp", SEQ),
        P(),
        P(SEQ, None),
        P(SEQ, None, None),
        P(SEQ, None, None),
        P(SEQ, None, None),
    )
    return jax.shard_map(
        shards, mesh=fine, in_specs=placed, out_specs=P(("dp",) + SEQ, None), check_vma=False
    )
```

```python
import jax
import jax.numpy as jnp
from jax import lax
from jax.sharding import PartitionSpec as P

SEQ = ("sy", "sx", "sc")
CHIP_AXES = ("sy", "sx")
CORE_AXIS = "sc"
CHUNKS = 1
RADIX = 4
SCATTER_PIECES = 1


def pack(state, ending):
    heads, rows, width = state.shape
    wide, parts = ending, []
    for _ in range(3):
        part = lax.reduce_precision(wide, exponent_bits=8, mantissa_bits=7)
        parts.append(part.astype(jnp.bfloat16))
        wide = wide - part
    block = jnp.pad(jnp.stack(parts, axis=1), ((0, 0), (0, width - 3)))
    return jnp.concatenate(
        [state.astype(jnp.bfloat16).reshape(heads * rows, width), block], axis=0
    )


def unpack(message, heads):
    width = message.shape[1]
    body = message[: heads * width].reshape(heads, width, width).astype(jnp.float32)
    tail = message[heads * width :, :3].astype(jnp.float32)
    return body, tail[:, 0] + tail[:, 1] + tail[:, 2]


def combine(earlier, latter):
    return (earlier[0] * jnp.exp(latter[1])[:, None, None] + latter[0], earlier[1] + latter[1])


def exclusive_scan(state, ending, axis, rider):
    count = lax.axis_size(axis)
    heads = state.shape[0]

    def fetch(pair, distance):
        pairs = [(j, j + distance) for j in range(count - distance)]
        return unpack(lax.ppermute(pack(*pair), axis, pairs), heads)

    covered = (state, ending)
    reach = 1
    while reach * RADIX < count:
        gathered = covered
        for multiple in range(1, RADIX):
            gathered = combine(fetch(covered, multiple * reach), gathered)
        covered = gathered
        if reach == 1:
            covered, rider = lax.optimization_barrier((covered, rider))
        reach *= RADIX
    if count == 1:
        return jnp.zeros_like(state), rider
    near = fetch(covered, 1)
    distance = 1 + reach
    while distance < count:
        near = combine(fetch(covered, distance), near)
        distance += reach
    return near[0], rider


def carried_in(state, ending, rider):
    heads = state.shape[0]
    half = heads // 2
    swap = [(0, 1), (1, 0)]
    core = lax.axis_index(CORE_AXIS)
    first = core == 0
    other_state, other_ending = unpack(lax.ppermute(pack(state, ending), CORE_AXIS, swap), heads)
    lower = (jnp.where(first, state, other_state), jnp.where(first, ending, other_ending))
    upper = (jnp.where(first, other_state, state), jnp.where(first, other_ending, ending))
    chip_state, chip_ending = combine(lower, upper)
    mine, rider = exclusive_scan(
        lax.dynamic_slice_in_dim(chip_state, core * half, half, axis=0),
        lax.dynamic_slice_in_dim(chip_ending, core * half, half, axis=0),
        CHIP_AXES,
        rider,
    )
    theirs = lax.ppermute(mine.astype(jnp.bfloat16), CORE_AXIS, swap).astype(jnp.float32)
    before = jnp.where(
        first, jnp.concatenate([mine, theirs], axis=0), jnp.concatenate([theirs, mine], axis=0)
    )
    return jnp.where(first, before, combine((before, 0.0), lower)[0]), rider


def shards(
    queries,
    keys_in,
    values,
    stream,
    log_decay,
    token_index,
    route_weight,
    moe_gain,
    out_weight,
    gate_weight,
    up_weight,
    down_weight,
):
    length, model_width = queries.shape
    head_count = log_decay.shape[1]
    head_size = model_width // head_count
    scaling = head_size ** (-0.5)
    device = lax.axis_index(SEQ)
    query_heads = queries.reshape(length, head_count, head_size).transpose(1, 0, 2)
    key_heads = keys_in.reshape(length, head_count, head_size).transpose(1, 0, 2)
    value_heads = values.reshape(length, head_count, head_size).transpose(1, 0, 2)
    running = jnp.cumsum(log_decay, axis=0).T
    ending = running[:, -1]
    shrink = jnp.exp(ending[:, None] - running)
    key_scaled = (key_heads.astype(jnp.float32) * shrink[:, :, None]).astype(jnp.bfloat16)
    local_state = jnp.einsum(
        "hsd,hse->hde", key_scaled, value_heads, preferred_element_type=jnp.float32
    )
    incoming, out_weight = carried_in(local_state, ending, out_weight)
    scores = (
        jnp.einsum("htd,hsd->hts", query_heads, key_heads, preferred_element_type=jnp.float32)
        * scaling
    )
    spacing = running[:, :, None] - running[:, None, :]
    causal = jnp.arange(length)[:, None] >= jnp.arange(length)[None, :]
    decay_mask = jnp.where(causal[None], jnp.exp(jnp.minimum(spacing, 0.0)), 0.0)
    attend_weights = (scores * decay_mask).astype(jnp.bfloat16)
    within = jnp.einsum(
        "hts,hsd->htd", attend_weights, value_heads, preferred_element_type=jnp.float32
    )
    query_scaled = (
        query_heads.astype(jnp.float32) * (jnp.exp(running) * scaling)[:, :, None]
    ).astype(jnp.bfloat16)
    within, query_scaled = lax.optimization_barrier((within, query_scaled))
    across = jnp.einsum(
        "htd,hde->hte",
        query_scaled,
        incoming.astype(jnp.bfloat16),
        preferred_element_type=jnp.float32,
    )
    unnormed = within + across
    spread = jnp.mean(unnormed * unnormed, axis=2, keepdims=True)
    normed = (
        (unnormed * lax.rsqrt(spread + 1e-06))
        .astype(jnp.bfloat16)
        .transpose(1, 0, 2)
        .reshape(length, model_width)
    )
    attended = jnp.dot(
        normed,
        lax.all_gather(out_weight, SEQ, axis=0, tiled=True),
        preferred_element_type=jnp.float32,
    )
    residual = (stream.astype(jnp.float32) + attended).astype(jnp.bfloat16)
    widened = residual.astype(jnp.float32)
    mixed_in = (
        widened * lax.rsqrt(jnp.mean(widened * widened, axis=1, keepdims=True) + 1e-06) * moe_gain
    ).astype(jnp.bfloat16)
    offsets = (token_index - device * length).reshape(-1)
    positions = jnp.arange(length)
    choose = (offsets[:, None] == positions[None, :]).astype(jnp.bfloat16)
    picked = jnp.dot(choose, mixed_in, preferred_element_type=jnp.float32).astype(jnp.bfloat16)
    picked = picked.reshape(token_index.shape + (model_width,))
    spread_weight = jnp.where(
        positions[:, None] == offsets[None, :], route_weight.reshape(-1)[None, :], 0.0
    ).reshape((length,) + token_index.shape)
    slots = token_index.shape[1]
    step = slots // CHUNKS
    total = widened
    for chunk in range(CHUNKS):
        window = slice(chunk * step, (chunk + 1) * step)
        arrived = lax.all_to_all(picked[:, window], SEQ, split_axis=0, concat_axis=0, tiled=True)
        gating = jnp.einsum(
            "snd,df->snf", arrived, gate_weight[0], preferred_element_type=jnp.float32
        )
        upward = jnp.einsum("snd,df->snf", arrived, up_weight[0], preferred_element_type=jnp.float32)
        activated = (jax.nn.silu(gating) * upward).astype(jnp.bfloat16)
        produced = jnp.einsum(
            "snf,fd->snd", activated, down_weight[0], preferred_element_type=jnp.float32
        ).astype(jnp.bfloat16)
        returned = lax.all_to_all(produced, SEQ, split_axis=0, concat_axis=0, tiled=True)
        flat_returned = returned.reshape(-1, model_width)
        remaining = spread_weight[:, :, window].reshape(length, -1)
        for _ in range(SCATTER_PIECES):
            part = lax.reduce_precision(remaining, exponent_bits=8, mantissa_bits=7)
            total = total + jnp.dot(
                part.astype(jnp.bfloat16), flat_returned, preferred_element_type=jnp.float32
            )
            remaining = remaining - part
    return total.astype(jnp.bfloat16)


def solution(mesh):
    fine = jax.sharding.Mesh(
        mesh.devices.reshape(mesh.shape["dp"], 4, -1, 2),
        ("dp",) + SEQ,
    )
    placed = (
        P(("dp",) + SEQ, None),
        P(("dp",) + SEQ, None),
        P(("dp",) + SEQ, None),
        P(("dp",) + SEQ, None),
        P(("dp",) + SEQ, None),
        P("dp", SEQ),
        P("dp", SEQ),
        P(),
        P(SEQ, None),
        P(SEQ, None, None),
        P(SEQ, None, None),
        P(SEQ, None, None),
    )
    return jax.shard_map(
        shards, mesh=fine, in_specs=placed, out_specs=P(("dp",) + SEQ, None), check_vma=False
    )
```

```python
import jax
import jax.numpy as jnp
from jax import lax
from jax.sharding import PartitionSpec as P

SEQ = ("sy", "sx", "sc")
CHIP_AXES = ("sy", "sx")
CORE_AXIS = "sc"
CHUNKS = 1
SCATTER_PIECES = 1


def pack(state, ending):
    heads, rows, width = state.shape
    wide, parts = ending, []
    for _ in range(3):
        part = lax.reduce_precision(wide, exponent_bits=8, mantissa_bits=7)
        parts.append(part.astype(jnp.bfloat16))
        wide = wide - part
    block = jnp.pad(jnp.stack(parts, axis=1), ((0, 0), (0, width - 3)))
    return jnp.concatenate(
        [state.astype(jnp.bfloat16).reshape(heads * rows, width), block], axis=0
    )


def unpack(message, heads):
    width = message.shape[1]
    body = message[: heads * width].reshape(heads, width, width).astype(jnp.float32)
    tail = message[heads * width :, :3].astype(jnp.float32)
    return body, tail[:, 0] + tail[:, 1] + tail[:, 2]


def combine(earlier, latter):
    return (earlier[0] * jnp.exp(latter[1])[:, None, None] + latter[0], earlier[1] + latter[1])


def exclusive_scan(state, ending, axis, rider):
    count = lax.axis_size(axis)
    heads = state.shape[0]

    def fetch(pair, distance):
        pairs = [(j, j + distance) for j in range(count - distance)]
        return unpack(lax.ppermute(pack(*pair), axis, pairs), heads)

    covered = (state, ending)
    reach = 1
    while 2 * reach < count:
        covered = combine(fetch(covered, reach), covered)
        if reach == 1:
            covered, rider = lax.optimization_barrier((covered, rider))
        reach *= 2
    if count == 1:
        return jnp.zeros_like(state), rider
    near = fetch(covered, 1)
    if reach + 1 < count:
        near = combine(fetch(covered, reach + 1), near)
    return near[0], rider


def carried_in(state, ending, rider):
    heads = state.shape[0]
    half = heads // 2
    swap = [(0, 1), (1, 0)]
    core = lax.axis_index(CORE_AXIS)
    first = core == 0
    other_state, other_ending = unpack(lax.ppermute(pack(state, ending), CORE_AXIS, swap), heads)
    lower = (jnp.where(first, state, other_state), jnp.where(first, ending, other_ending))
    upper = (jnp.where(first, other_state, state), jnp.where(first, other_ending, ending))
    chip_state, chip_ending = combine(lower, upper)
    mine, rider = exclusive_scan(
        lax.dynamic_slice_in_dim(chip_state, core * half, half, axis=0),
        lax.dynamic_slice_in_dim(chip_ending, core * half, half, axis=0),
        CHIP_AXES,
        rider,
    )
    theirs = lax.ppermute(mine.astype(jnp.bfloat16), CORE_AXIS, swap).astype(jnp.float32)
    before = jnp.where(
        first, jnp.concatenate([mine, theirs], axis=0), jnp.concatenate([theirs, mine], axis=0)
    )
    return jnp.where(first, before, combine((before, 0.0), lower)[0]), rider


def shards(
    queries,
    keys_in,
    values,
    stream,
    log_decay,
    token_index,
    route_weight,
    moe_gain,
    out_weight,
    gate_weight,
    up_weight,
    down_weight,
):
    length, model_width = queries.shape
    head_count = log_decay.shape[1]
    head_size = model_width // head_count
    scaling = head_size ** (-0.5)
    device = lax.axis_index(SEQ)
    query_heads = queries.reshape(length, head_count, head_size).transpose(1, 0, 2)
    key_heads = keys_in.reshape(length, head_count, head_size).transpose(1, 0, 2)
    value_heads = values.reshape(length, head_count, head_size).transpose(1, 0, 2)
    running = jnp.cumsum(log_decay, axis=0).T
    ending = running[:, -1]
    shrink = jnp.exp(ending[:, None] - running)
    key_scaled = (key_heads.astype(jnp.float32) * shrink[:, :, None]).astype(jnp.bfloat16)
    local_state = jnp.einsum(
        "hsd,hse->hde", key_scaled, value_heads, preferred_element_type=jnp.float32
    )
    query_scaled = (
        query_heads.astype(jnp.float32) * (jnp.exp(running) * scaling)[:, :, None]
    ).astype(jnp.bfloat16)
    incoming, (out_weight, query_scaled) = carried_in(
        local_state, ending, (out_weight, query_scaled)
    )
    scores = (
        jnp.einsum("htd,hsd->hts", query_heads, key_heads, preferred_element_type=jnp.float32)
        * scaling
    )
    spacing = running[:, :, None] - running[:, None, :]
    causal = jnp.arange(length)[:, None] >= jnp.arange(length)[None, :]
    decay_mask = jnp.where(causal[None], jnp.exp(jnp.minimum(spacing, 0.0)), 0.0)
    attend_weights = (scores * decay_mask).astype(jnp.bfloat16)
    within = jnp.einsum(
        "hts,hsd->htd", attend_weights, value_heads, preferred_element_type=jnp.float32
    )
    within, query_scaled = lax.optimization_barrier((within, query_scaled))
    across = jnp.einsum(
        "htd,hde->hte",
        query_scaled,
        incoming.astype(jnp.bfloat16),
        preferred_element_type=jnp.float32,
    )
    unnormed = within + across
    spread = jnp.mean(unnormed * unnormed, axis=2, keepdims=True)
    normed = (
        (unnormed * lax.rsqrt(spread + 1e-06))
        .astype(jnp.bfloat16)
        .transpose(1, 0, 2)
        .reshape(length, model_width)
    )
    attended = jnp.dot(
        normed,
        lax.all_gather(out_weight, SEQ, axis=0, tiled=True),
        preferred_element_type=jnp.float32,
    )
    residual = (stream.astype(jnp.float32) + attended).astype(jnp.bfloat16)
    widened = residual.astype(jnp.float32)
    mixed_in = (
        widened * lax.rsqrt(jnp.mean(widened * widened, axis=1, keepdims=True) + 1e-06) * moe_gain
    ).astype(jnp.bfloat16)
    offsets = (token_index - device * length).reshape(-1)
    positions = jnp.arange(length)
    choose = (offsets[:, None] == positions[None, :]).astype(jnp.bfloat16)
    picked = jnp.dot(choose, mixed_in, preferred_element_type=jnp.float32).astype(jnp.bfloat16)
    picked = picked.reshape(token_index.shape + (model_width,))
    spread_weight = jnp.where(
        positions[:, None] == offsets[None, :], route_weight.reshape(-1)[None, :], 0.0
    ).reshape((length,) + token_index.shape)
    slots = token_index.shape[1]
    step = slots // CHUNKS
    total = widened
    for chunk in range(CHUNKS):
        window = slice(chunk * step, (chunk + 1) * step)
        arrived = lax.all_to_all(picked[:, window], SEQ, split_axis=0, concat_axis=0, tiled=True)
        gating = jnp.einsum(
            "snd,df->snf", arrived, gate_weight[0], preferred_element_type=jnp.float32
        )
        upward = jnp.einsum("snd,df->snf", arrived, up_weight[0], preferred_element_type=jnp.float32)
        activated = (jax.nn.silu(gating) * upward).astype(jnp.bfloat16)
        produced = jnp.einsum(
            "snf,fd->snd", activated, down_weight[0], preferred_element_type=jnp.float32
        ).astype(jnp.bfloat16)
        returned = lax.all_to_all(produced, SEQ, split_axis=0, concat_axis=0, tiled=True)
        flat_returned = returned.reshape(-1, model_width)
        remaining = spread_weight[:, :, window].reshape(length, -1)
        for _ in range(SCATTER_PIECES):
            part = lax.reduce_precision(remaining, exponent_bits=8, mantissa_bits=7)
            total = total + jnp.dot(
                part.astype(jnp.bfloat16), flat_returned, preferred_element_type=jnp.float32
            )
            remaining = remaining - part
    return total.astype(jnp.bfloat16)


def solution(mesh):
    fine = jax.sharding.Mesh(
        mesh.devices.reshape(mesh.shape["dp"], 4, -1, 2),
        ("dp",) + SEQ,
    )
    placed = (
        P(("dp",) + SEQ, None),
        P(("dp",) + SEQ, None),
        P(("dp",) + SEQ, None),
        P(("dp",) + SEQ, None),
        P(("dp",) + SEQ, None),
        P("dp", SEQ),
        P("dp", SEQ),
        P(),
        P(SEQ, None),
        P(SEQ, None, None),
        P(SEQ, None, None),
        P(SEQ, None, None),
    )
    return jax.shard_map(
        shards, mesh=fine, in_specs=placed, out_specs=P(("dp",) + SEQ, None), check_vma=False
    )
```

```python
import jax
import jax.numpy as jnp
from jax import lax
from jax.sharding import PartitionSpec as P

SEQ = ("sy", "sx", "sc")
CHIP_AXES = ("sy", "sx")
CORE_AXIS = "sc"
CHUNKS = 1
SCATTER_PIECES = 1


def pack(state, ending):
    heads, rows, width = state.shape
    wide, parts = ending, []
    for _ in range(3):
        part = lax.reduce_precision(wide, exponent_bits=8, mantissa_bits=7)
        parts.append(part.astype(jnp.bfloat16))
        wide = wide - part
    block = jnp.pad(jnp.stack(parts, axis=1), ((0, 0), (0, width - 3)))
    return jnp.concatenate(
        [state.astype(jnp.bfloat16).reshape(heads * rows, width), block], axis=0
    )


def unpack(message, heads):
    width = message.shape[1]
    body = message[: heads * width].reshape(heads, width, width).astype(jnp.float32)
    tail = message[heads * width :, :3].astype(jnp.float32)
    return body, tail[:, 0] + tail[:, 1] + tail[:, 2]


def combine(earlier, latter):
    return (earlier[0] * jnp.exp(latter[1])[:, None, None] + latter[0], earlier[1] + latter[1])


def exclusive_scan(state, ending, axis, rider):
    count = lax.axis_size(axis)
    heads = state.shape[0]

    def fetch(pair, distance):
        pairs = [(j, j + distance) for j in range(count - distance)]
        return unpack(lax.ppermute(pack(*pair), axis, pairs), heads)

    covered = (state, ending)
    reach = 1
    while 2 * reach < count:
        covered = combine(fetch(covered, reach), covered)
        if reach == 1:
            covered, rider = lax.optimization_barrier((covered, rider))
        reach *= 2
    if count == 1:
        return jnp.zeros_like(state), rider
    near = fetch(covered, 1)
    if reach + 1 < count:
        near = combine(fetch(covered, reach + 1), near)
    return near[0], rider


def carried_in(state, ending, rider):
    heads = state.shape[0]
    half = heads // 2
    swap = [(0, 1), (1, 0)]
    core = lax.axis_index(CORE_AXIS)
    first = core == 0
    other_state, other_ending = unpack(lax.ppermute(pack(state, ending), CORE_AXIS, swap), heads)
    lower = (jnp.where(first, state, other_state), jnp.where(first, ending, other_ending))
    upper = (jnp.where(first, other_state, state), jnp.where(first, other_ending, ending))
    chip_state, chip_ending = combine(lower, upper)
    mine, rider = exclusive_scan(
        lax.dynamic_slice_in_dim(chip_state, core * half, half, axis=0),
        lax.dynamic_slice_in_dim(chip_ending, core * half, half, axis=0),
        CHIP_AXES,
        rider,
    )
    theirs = lax.ppermute(mine.astype(jnp.bfloat16), CORE_AXIS, swap).astype(jnp.float32)
    before = jnp.where(
        first, jnp.concatenate([mine, theirs], axis=0), jnp.concatenate([theirs, mine], axis=0)
    )
    return jnp.where(first, before, combine((before, 0.0), lower)[0]), rider


def shards(
    queries,
    keys_in,
    values,
    stream,
    log_decay,
    token_index,
    route_weight,
    moe_gain,
    out_weight,
    gate_weight,
    up_weight,
    down_weight,
):
    length, model_width = queries.shape
    head_count = log_decay.shape[1]
    head_size = model_width // head_count
    scaling = head_size ** (-0.5)
    device = lax.axis_index(SEQ)
    query_heads = queries.reshape(length, head_count, head_size).transpose(1, 0, 2)
    key_heads = keys_in.reshape(length, head_count, head_size).transpose(1, 0, 2)
    value_heads = values.reshape(length, head_count, head_size).transpose(1, 0, 2)
    running = jnp.cumsum(log_decay, axis=0).T
    ending = running[:, -1]
    shrink = jnp.exp(ending[:, None] - running)
    key_scaled = (key_heads.astype(jnp.float32) * shrink[:, :, None]).astype(jnp.bfloat16)
    local_state = jnp.einsum(
        "hsd,hse->hde", key_scaled, value_heads, preferred_element_type=jnp.float32
    )
    planes, rows_count = lax.axis_size("dp"), lax.axis_size("sy")
    plane, row = lax.axis_index("dp"), lax.axis_index("sy")
    turned = [
        (z * rows_count + (y + z) % rows_count, z * rows_count + y)
        for z in range(planes)
        for y in range(rows_count)
    ]
    shifted = lax.ppermute(out_weight, ("dp", "sy"), turned)
    row_block = lax.all_gather(shifted, ("sx", "sc"), axis=0, tiled=True)
    blocks = lax.all_gather(row_block, "dp", axis=0)
    incoming, _ = carried_in(local_state, ending, ending)
    scores = (
        jnp.einsum("htd,hsd->hts", query_heads, key_heads, preferred_element_type=jnp.float32)
        * scaling
    )
    spacing = running[:, :, None] - running[:, None, :]
    causal = jnp.arange(length)[:, None] >= jnp.arange(length)[None, :]
    decay_mask = jnp.where(causal[None], jnp.exp(jnp.minimum(spacing, 0.0)), 0.0)
    attend_weights = (scores * decay_mask).astype(jnp.bfloat16)
    within = jnp.einsum(
        "hts,hsd->htd", attend_weights, value_heads, preferred_element_type=jnp.float32
    )
    query_scaled = (
        query_heads.astype(jnp.float32) * (jnp.exp(running) * scaling)[:, :, None]
    ).astype(jnp.bfloat16)
    within, query_scaled = lax.optimization_barrier((within, query_scaled))
    across = jnp.einsum(
        "htd,hde->hte",
        query_scaled,
        incoming.astype(jnp.bfloat16),
        preferred_element_type=jnp.float32,
    )
    unnormed = within + across
    spread = jnp.mean(unnormed * unnormed, axis=2, keepdims=True)
    normed = (
        (unnormed * lax.rsqrt(spread + 1e-06))
        .astype(jnp.bfloat16)
        .transpose(1, 0, 2)
        .reshape(length, model_width)
    )
    rolled = jnp.roll(normed.reshape(length, planes, -1), -row, axis=1)
    attended = jnp.einsum("tzk,zkd->td", rolled, blocks, preferred_element_type=jnp.float32)
    residual = (stream.astype(jnp.float32) + attended).astype(jnp.bfloat16)
    widened = residual.astype(jnp.float32)
    mixed_in = (
        widened * lax.rsqrt(jnp.mean(widened * widened, axis=1, keepdims=True) + 1e-06) * moe_gain
    ).astype(jnp.bfloat16)
    offsets = (token_index - device * length).reshape(-1)
    positions = jnp.arange(length)
    choose = (offsets[:, None] == positions[None, :]).astype(jnp.bfloat16)
    picked = jnp.dot(choose, mixed_in, preferred_element_type=jnp.float32).astype(jnp.bfloat16)
    picked = picked.reshape(token_index.shape + (model_width,))
    spread_weight = jnp.where(
        positions[:, None] == offsets[None, :], route_weight.reshape(-1)[None, :], 0.0
    ).reshape((length,) + token_index.shape)
    slots = token_index.shape[1]
    step = slots // CHUNKS
    total = widened
    for chunk in range(CHUNKS):
        window = slice(chunk * step, (chunk + 1) * step)
        arrived = lax.all_to_all(picked[:, window], SEQ, split_axis=0, concat_axis=0, tiled=True)
        gating = jnp.einsum(
            "snd,df->snf", arrived, gate_weight[0], preferred_element_type=jnp.float32
        )
        upward = jnp.einsum("snd,df->snf", arrived, up_weight[0], preferred_element_type=jnp.float32)
        activated = (jax.nn.silu(gating) * upward).astype(jnp.bfloat16)
        produced = jnp.einsum(
            "snf,fd->snd", activated, down_weight[0], preferred_element_type=jnp.float32
        ).astype(jnp.bfloat16)
        returned = lax.all_to_all(produced, SEQ, split_axis=0, concat_axis=0, tiled=True)
        flat_returned = returned.reshape(-1, model_width)
        remaining = spread_weight[:, :, window].reshape(length, -1)
        for _ in range(SCATTER_PIECES):
            part = lax.reduce_precision(remaining, exponent_bits=8, mantissa_bits=7)
            total = total + jnp.dot(
                part.astype(jnp.bfloat16), flat_returned, preferred_element_type=jnp.float32
            )
            remaining = remaining - part
    return total.astype(jnp.bfloat16)


def solution(mesh):
    fine = jax.sharding.Mesh(
        mesh.devices.reshape(mesh.shape["dp"], 4, -1, 2),
        ("dp",) + SEQ,
    )
    placed = (
        P(("dp",) + SEQ, None),
        P(("dp",) + SEQ, None),
        P(("dp",) + SEQ, None),
        P(("dp",) + SEQ, None),
        P(("dp",) + SEQ, None),
        P("dp", SEQ),
        P("dp", SEQ),
        P(),
        P(SEQ, None),
        P(SEQ, None, None),
        P(SEQ, None, None),
        P(SEQ, None, None),
    )
    return jax.shard_map(
        shards, mesh=fine, in_specs=placed, out_specs=P(("dp",) + SEQ, None), check_vma=False
    )
```

```python
import jax
import jax.numpy as jnp
from jax import lax
from jax.sharding import PartitionSpec as P

SEQ = ("sy", "sx", "sc")
CHIP_AXES = ("sy", "sx")
CORE_AXIS = "sc"
CHUNKS = 1
SCATTER_PIECES = 1


def pack(state, ending):
    heads, rows, width = state.shape
    wide, parts = ending, []
    for _ in range(3):
        part = lax.reduce_precision(wide, exponent_bits=8, mantissa_bits=7)
        parts.append(part.astype(jnp.bfloat16))
        wide = wide - part
    block = jnp.pad(jnp.stack(parts, axis=1), ((0, 0), (0, width - 3)))
    return jnp.concatenate(
        [state.astype(jnp.bfloat16).reshape(heads * rows, width), block], axis=0
    )


def unpack(message, heads):
    width = message.shape[1]
    body = message[: heads * width].reshape(heads, width, width).astype(jnp.float32)
    tail = message[heads * width :, :3].astype(jnp.float32)
    return body, tail[:, 0] + tail[:, 1] + tail[:, 2]


def combine(earlier, latter):
    return (earlier[0] * jnp.exp(latter[1])[:, None, None] + latter[0], earlier[1] + latter[1])


def exclusive_scan(state, ending, axis, rider):
    count = lax.axis_size(axis)
    heads = state.shape[0]

    def fetch(pair, distance):
        pairs = [(j, j + distance) for j in range(count - distance)]
        return unpack(lax.ppermute(pack(*pair), axis, pairs), heads)

    covered = (state, ending)
    reach = 1
    while 2 * reach < count:
        covered = combine(fetch(covered, reach), covered)
        if reach == 1:
            covered, rider = lax.optimization_barrier((covered, rider))
        reach *= 2
    if count == 1:
        return jnp.zeros_like(state), rider
    near = fetch(covered, 1)
    if reach + 1 < count:
        near = combine(fetch(covered, reach + 1), near)
    return near[0], rider


def carried_in(state, ending, rider):
    heads = state.shape[0]
    swap = [(0, 1), (1, 0)]
    core = lax.axis_index(CORE_AXIS)
    first = core == 0
    other_state, other_ending = unpack(lax.ppermute(pack(state, ending), CORE_AXIS, swap), heads)
    lower = (jnp.where(first, state, other_state), jnp.where(first, ending, other_ending))
    upper = (jnp.where(first, other_state, state), jnp.where(first, other_ending, ending))
    chip_state, chip_ending = combine(lower, upper)
    before, rider = exclusive_scan(chip_state, chip_ending, CHIP_AXES, rider)
    return jnp.where(first, before, combine((before, 0.0), lower)[0]), rider


def shards(
    queries,
    keys_in,
    values,
    stream,
    log_decay,
    token_index,
    route_weight,
    moe_gain,
    out_weight,
    gate_weight,
    up_weight,
    down_weight,
):
    length, model_width = queries.shape
    head_count = log_decay.shape[1]
    head_size = model_width // head_count
    scaling = head_size ** (-0.5)
    device = lax.axis_index(SEQ)
    query_heads = queries.reshape(length, head_count, head_size).transpose(1, 0, 2)
    key_heads = keys_in.reshape(length, head_count, head_size).transpose(1, 0, 2)
    value_heads = values.reshape(length, head_count, head_size).transpose(1, 0, 2)
    running = jnp.cumsum(log_decay, axis=0).T
    ending = running[:, -1]
    shrink = jnp.exp(ending[:, None] - running)
    key_scaled = (key_heads.astype(jnp.float32) * shrink[:, :, None]).astype(jnp.bfloat16)
    local_state = jnp.einsum(
        "hsd,hse->hde", key_scaled, value_heads, preferred_element_type=jnp.float32
    )
    incoming, out_weight = carried_in(local_state, ending, out_weight)
    scores = (
        jnp.einsum("htd,hsd->hts", query_heads, key_heads, preferred_element_type=jnp.float32)
        * scaling
    )
    spacing = running[:, :, None] - running[:, None, :]
    causal = jnp.arange(length)[:, None] >= jnp.arange(length)[None, :]
    decay_mask = jnp.where(causal[None], jnp.exp(jnp.minimum(spacing, 0.0)), 0.0)
    attend_weights = (scores * decay_mask).astype(jnp.bfloat16)
    within = jnp.einsum(
        "hts,hsd->htd", attend_weights, value_heads, preferred_element_type=jnp.float32
    )
    query_scaled = (
        query_heads.astype(jnp.float32) * (jnp.exp(running) * scaling)[:, :, None]
    ).astype(jnp.bfloat16)
    within, query_scaled = lax.optimization_barrier((within, query_scaled))
    across = jnp.einsum(
        "htd,hde->hte",
        query_scaled,
        incoming.astype(jnp.bfloat16),
        preferred_element_type=jnp.float32,
    )
    unnormed = within + across
    spread = jnp.mean(unnormed * unnormed, axis=2, keepdims=True)
    normed = (
        (unnormed * lax.rsqrt(spread + 1e-06))
        .astype(jnp.bfloat16)
        .transpose(1, 0, 2)
        .reshape(length, model_width)
    )
    attended = jnp.dot(
        normed,
        lax.all_gather(out_weight, SEQ, axis=0, tiled=True),
        preferred_element_type=jnp.float32,
    )
    residual = (stream.astype(jnp.float32) + attended).astype(jnp.bfloat16)
    widened = residual.astype(jnp.float32)
    mixed_in = (
        widened * lax.rsqrt(jnp.mean(widened * widened, axis=1, keepdims=True) + 1e-06) * moe_gain
    ).astype(jnp.bfloat16)
    offsets = (token_index - device * length).reshape(-1)
    positions = jnp.arange(length)
    choose = (offsets[:, None] == positions[None, :]).astype(jnp.bfloat16)
    picked = jnp.dot(choose, mixed_in, preferred_element_type=jnp.float32).astype(jnp.bfloat16)
    picked = picked.reshape(token_index.shape + (model_width,))
    spread_weight = jnp.where(
        positions[:, None] == offsets[None, :], route_weight.reshape(-1)[None, :], 0.0
    ).reshape((length,) + token_index.shape)
    slots = token_index.shape[1]
    step = slots // CHUNKS
    total = widened
    for chunk in range(CHUNKS):
        window = slice(chunk * step, (chunk + 1) * step)
        arrived = lax.all_to_all(picked[:, window], SEQ, split_axis=0, concat_axis=0, tiled=True)
        gating = jnp.einsum(
            "snd,df->snf", arrived, gate_weight[0], preferred_element_type=jnp.float32
        )
        upward = jnp.einsum("snd,df->snf", arrived, up_weight[0], preferred_element_type=jnp.float32)
        activated = (jax.nn.silu(gating) * upward).astype(jnp.bfloat16)
        produced = jnp.einsum(
            "snf,fd->snd", activated, down_weight[0], preferred_element_type=jnp.float32
        ).astype(jnp.bfloat16)
        returned = lax.all_to_all(produced, SEQ, split_axis=0, concat_axis=0, tiled=True)
        flat_returned = returned.reshape(-1, model_width)
        remaining = spread_weight[:, :, window].reshape(length, -1)
        for _ in range(SCATTER_PIECES):
            part = lax.reduce_precision(remaining, exponent_bits=8, mantissa_bits=7)
            total = total + jnp.dot(
                part.astype(jnp.bfloat16), flat_returned, preferred_element_type=jnp.float32
            )
            remaining = remaining - part
    return total.astype(jnp.bfloat16)


def solution(mesh):
    fine = jax.sharding.Mesh(
        mesh.devices.reshape(mesh.shape["dp"], 4, -1, 2),
        ("dp",) + SEQ,
    )
    placed = (
        P(("dp",) + SEQ, None),
        P(("dp",) + SEQ, None),
        P(("dp",) + SEQ, None),
        P(("dp",) + SEQ, None),
        P(("dp",) + SEQ, None),
        P("dp", SEQ),
        P("dp", SEQ),
        P(),
        P(SEQ, None),
        P(SEQ, None, None),
        P(SEQ, None, None),
        P(SEQ, None, None),
    )
    return jax.shard_map(
        shards, mesh=fine, in_specs=placed, out_specs=P(("dp",) + SEQ, None), check_vma=False
    )
```

```python
import jax
import jax.numpy as jnp
from jax import lax
from jax.sharding import PartitionSpec as P

SEQ = ("sy", "sx", "sc")
CHIP_AXES = ("sy", "sx")
CORE_AXIS = "sc"
CHUNKS = 1
SCATTER_PIECES = 1


def pack(state, ending):
    heads, rows, width = state.shape
    wide, parts = ending, []
    for _ in range(3):
        part = lax.reduce_precision(wide, exponent_bits=8, mantissa_bits=7)
        parts.append(part.astype(jnp.bfloat16))
        wide = wide - part
    block = jnp.pad(jnp.stack(parts, axis=1), ((0, 0), (0, width - 3)))
    return jnp.concatenate(
        [state.astype(jnp.bfloat16).reshape(heads * rows, width), block], axis=0
    )


def unpack(message, heads):
    width = message.shape[1]
    body = message[: heads * width].reshape(heads, width, width).astype(jnp.float32)
    tail = message[heads * width :, :3].astype(jnp.float32)
    return body, tail[:, 0] + tail[:, 1] + tail[:, 2]


def combine(earlier, latter):
    return (earlier[0] * jnp.exp(latter[1])[:, None, None] + latter[0], earlier[1] + latter[1])


def exclusive_scan(state, ending, axis, rider):
    count = lax.axis_size(axis)
    heads = state.shape[0]

    def fetch(pair, distance):
        pairs = [(j, j + distance) for j in range(count - distance)]
        return unpack(lax.ppermute(pack(*pair), axis, pairs), heads)

    covered = (state, ending)
    reach = 1
    while 2 * reach < count:
        covered = combine(fetch(covered, reach), covered)
        if reach == 2:
            covered, rider = lax.optimization_barrier((covered, rider))
        reach *= 2
    if count == 1:
        return jnp.zeros_like(state), rider
    near = fetch(covered, 1)
    if reach + 1 < count:
        near = combine(fetch(covered, reach + 1), near)
    return near[0], rider


def carried_in(state, ending, rider):
    heads = state.shape[0]
    half = heads // 2
    swap = [(0, 1), (1, 0)]
    core = lax.axis_index(CORE_AXIS)
    first = core == 0
    other_state, other_ending = unpack(lax.ppermute(pack(state, ending), CORE_AXIS, swap), heads)
    lower = (jnp.where(first, state, other_state), jnp.where(first, ending, other_ending))
    upper = (jnp.where(first, other_state, state), jnp.where(first, other_ending, ending))
    chip_state, chip_ending = combine(lower, upper)
    mine, rider = exclusive_scan(
        lax.dynamic_slice_in_dim(chip_state, core * half, half, axis=0),
        lax.dynamic_slice_in_dim(chip_ending, core * half, half, axis=0),
        CHIP_AXES,
        rider,
    )
    theirs = lax.ppermute(mine.astype(jnp.bfloat16), CORE_AXIS, swap).astype(jnp.float32)
    before = jnp.where(
        first, jnp.concatenate([mine, theirs], axis=0), jnp.concatenate([theirs, mine], axis=0)
    )
    return jnp.where(first, before, combine((before, 0.0), lower)[0]), rider


def shards(
    queries,
    keys_in,
    values,
    stream,
    log_decay,
    token_index,
    route_weight,
    moe_gain,
    out_weight,
    gate_weight,
    up_weight,
    down_weight,
):
    length, model_width = queries.shape
    head_count = log_decay.shape[1]
    head_size = model_width // head_count
    scaling = head_size ** (-0.5)
    device = lax.axis_index(SEQ)
    query_heads = queries.reshape(length, head_count, head_size).transpose(1, 0, 2)
    key_heads = keys_in.reshape(length, head_count, head_size).transpose(1, 0, 2)
    value_heads = values.reshape(length, head_count, head_size).transpose(1, 0, 2)
    running = jnp.cumsum(log_decay, axis=0).T
    ending = running[:, -1]
    shrink = jnp.exp(ending[:, None] - running)
    key_scaled = (key_heads.astype(jnp.float32) * shrink[:, :, None]).astype(jnp.bfloat16)
    local_state = jnp.einsum(
        "hsd,hse->hde", key_scaled, value_heads, preferred_element_type=jnp.float32
    )
    incoming, out_weight = carried_in(local_state, ending, out_weight)
    scores = (
        jnp.einsum("htd,hsd->hts", query_heads, key_heads, preferred_element_type=jnp.float32)
        * scaling
    )
    spacing = running[:, :, None] - running[:, None, :]
    causal = jnp.arange(length)[:, None] >= jnp.arange(length)[None, :]
    decay_mask = jnp.where(causal[None], jnp.exp(jnp.minimum(spacing, 0.0)), 0.0)
    attend_weights = (scores * decay_mask).astype(jnp.bfloat16)
    within = jnp.einsum(
        "hts,hsd->htd", attend_weights, value_heads, preferred_element_type=jnp.float32
    )
    query_scaled = (
        query_heads.astype(jnp.float32) * (jnp.exp(running) * scaling)[:, :, None]
    ).astype(jnp.bfloat16)
    within, query_scaled = lax.optimization_barrier((within, query_scaled))
    across = jnp.einsum(
        "htd,hde->hte",
        query_scaled,
        incoming.astype(jnp.bfloat16),
        preferred_element_type=jnp.float32,
    )
    unnormed = within + across
    spread = jnp.mean(unnormed * unnormed, axis=2, keepdims=True)
    normed = (
        (unnormed * lax.rsqrt(spread + 1e-06))
        .astype(jnp.bfloat16)
        .transpose(1, 0, 2)
        .reshape(length, model_width)
    )
    attended = jnp.dot(
        normed,
        lax.all_gather(out_weight, SEQ, axis=0, tiled=True),
        preferred_element_type=jnp.float32,
    )
    residual = (stream.astype(jnp.float32) + attended).astype(jnp.bfloat16)
    widened = residual.astype(jnp.float32)
    mixed_in = (
        widened * lax.rsqrt(jnp.mean(widened * widened, axis=1, keepdims=True) + 1e-06) * moe_gain
    ).astype(jnp.bfloat16)
    offsets = (token_index - device * length).reshape(-1)
    positions = jnp.arange(length)
    choose = (offsets[:, None] == positions[None, :]).astype(jnp.bfloat16)
    picked = jnp.dot(choose, mixed_in, preferred_element_type=jnp.float32).astype(jnp.bfloat16)
    picked = picked.reshape(token_index.shape + (model_width,))
    spread_weight = jnp.where(
        positions[:, None] == offsets[None, :], route_weight.reshape(-1)[None, :], 0.0
    ).reshape((length,) + token_index.shape)
    slots = token_index.shape[1]
    step = slots // CHUNKS
    total = widened
    for chunk in range(CHUNKS):
        window = slice(chunk * step, (chunk + 1) * step)
        arrived = lax.all_to_all(picked[:, window], SEQ, split_axis=0, concat_axis=0, tiled=True)
        gating = jnp.einsum(
            "snd,df->snf", arrived, gate_weight[0], preferred_element_type=jnp.float32
        )
        upward = jnp.einsum("snd,df->snf", arrived, up_weight[0], preferred_element_type=jnp.float32)
        activated = (jax.nn.silu(gating) * upward).astype(jnp.bfloat16)
        produced = jnp.einsum(
            "snf,fd->snd", activated, down_weight[0], preferred_element_type=jnp.float32
        ).astype(jnp.bfloat16)
        returned = lax.all_to_all(produced, SEQ, split_axis=0, concat_axis=0, tiled=True)
        flat_returned = returned.reshape(-1, model_width)
        remaining = spread_weight[:, :, window].reshape(length, -1)
        for _ in range(SCATTER_PIECES):
            part = lax.reduce_precision(remaining, exponent_bits=8, mantissa_bits=7)
            total = total + jnp.dot(
                part.astype(jnp.bfloat16), flat_returned, preferred_element_type=jnp.float32
            )
            remaining = remaining - part
    return total.astype(jnp.bfloat16)


def solution(mesh):
    fine = jax.sharding.Mesh(
        mesh.devices.reshape(mesh.shape["dp"], 4, -1, 2),
        ("dp",) + SEQ,
    )
    placed = (
        P(("dp",) + SEQ, None),
        P(("dp",) + SEQ, None),
        P(("dp",) + SEQ, None),
        P(("dp",) + SEQ, None),
        P(("dp",) + SEQ, None),
        P("dp", SEQ),
        P("dp", SEQ),
        P(),
        P(SEQ, None),
        P(SEQ, None, None),
        P(SEQ, None, None),
        P(SEQ, None, None),
    )
    return jax.shard_map(
        shards, mesh=fine, in_specs=placed, out_specs=P(("dp",) + SEQ, None), check_vma=False
    )
```

```python
import jax
import jax.numpy as jnp
from jax import lax
from jax.sharding import PartitionSpec as P

SEQ = ("sy", "sx", "sc")
CHIP_AXES = ("sy", "sx")
CORE_AXIS = "sc"
CHUNKS = 1
SCATTER_PIECES = 1


def pack(state, ending):
    heads, rows, width = state.shape
    wide, parts = ending, []
    for _ in range(3):
        part = lax.reduce_precision(wide, exponent_bits=8, mantissa_bits=7)
        parts.append(part.astype(jnp.bfloat16))
        wide = wide - part
    block = jnp.pad(jnp.stack(parts, axis=1), ((0, 0), (0, width - 3)))
    return jnp.concatenate(
        [state.astype(jnp.bfloat16).reshape(heads * rows, width), block], axis=0
    )


def unpack(message, heads):
    width = message.shape[1]
    body = message[: heads * width].reshape(heads, width, width).astype(jnp.float32)
    tail = message[heads * width :, :3].astype(jnp.float32)
    return body, tail[:, 0] + tail[:, 1] + tail[:, 2]


def combine(earlier, latter):
    return (earlier[0] * jnp.exp(latter[1])[:, None, None] + latter[0], earlier[1] + latter[1])


def exclusive_scan(state, ending, axis, rider):
    count = lax.axis_size(axis)
    heads = state.shape[0]

    def fetch(pair, distance):
        pairs = [(j, j + distance) for j in range(count - distance)]
        return unpack(lax.ppermute(pack(*pair), axis, pairs), heads)

    covered = (state, ending)
    reach = 1
    while 2 * reach < count:
        covered = combine(fetch(covered, reach), covered)
        if reach == 1:
            covered, rider = lax.optimization_barrier((covered, rider))
        reach *= 2
    if count == 1:
        return jnp.zeros_like(state), rider
    near = fetch(covered, 1)
    if reach + 1 < count:
        near = combine(fetch(covered, reach + 1), near)
    return near[0], rider


def carried_in(state, ending, rider):
    heads = state.shape[0]
    half = heads // 2
    swap = [(0, 1), (1, 0)]
    core = lax.axis_index(CORE_AXIS)
    first = core == 0
    other_state, other_ending = unpack(lax.ppermute(pack(state, ending), CORE_AXIS, swap), heads)
    lower = (jnp.where(first, state, other_state), jnp.where(first, ending, other_ending))
    upper = (jnp.where(first, other_state, state), jnp.where(first, other_ending, ending))
    chip_state, chip_ending = combine(lower, upper)
    mine, rider = exclusive_scan(
        lax.dynamic_slice_in_dim(chip_state, core * half, half, axis=0),
        lax.dynamic_slice_in_dim(chip_ending, core * half, half, axis=0),
        CHIP_AXES,
        rider,
    )
    theirs = lax.ppermute(mine.astype(jnp.bfloat16), CORE_AXIS, swap).astype(jnp.float32)
    before = jnp.where(
        first, jnp.concatenate([mine, theirs], axis=0), jnp.concatenate([theirs, mine], axis=0)
    )
    return jnp.where(first, before, combine((before, 0.0), lower)[0]), rider


def shards(
    queries,
    keys_in,
    values,
    stream,
    log_decay,
    token_index,
    route_weight,
    moe_gain,
    out_weight,
    gate_weight,
    up_weight,
    down_weight,
):
    length, model_width = queries.shape
    head_count = log_decay.shape[1]
    head_size = model_width // head_count
    scaling = head_size ** (-0.5)
    device = lax.axis_index(SEQ)
    query_heads = queries.reshape(length, head_count, head_size).transpose(1, 0, 2)
    key_heads = keys_in.reshape(length, head_count, head_size).transpose(1, 0, 2)
    value_heads = values.reshape(length, head_count, head_size).transpose(1, 0, 2)
    running = jnp.cumsum(log_decay, axis=0).T
    ending = running[:, -1]
    shrink = jnp.exp(ending[:, None] - running)
    key_scaled = (key_heads.astype(jnp.float32) * shrink[:, :, None]).astype(jnp.bfloat16)
    local_state = jnp.einsum(
        "hsd,hse->hde", key_scaled, value_heads, preferred_element_type=jnp.float32
    )
    incoming, out_weight = carried_in(local_state, ending, out_weight)
    scores = (
        jnp.einsum("htd,hsd->hts", query_heads, key_heads, preferred_element_type=jnp.float32)
        * scaling
    )
    spacing = running[:, :, None] - running[:, None, :]
    causal = jnp.arange(length)[:, None] >= jnp.arange(length)[None, :]
    decay_mask = jnp.where(causal[None], jnp.exp(jnp.minimum(spacing, 0.0)), 0.0)
    attend_weights = (scores * decay_mask).astype(jnp.bfloat16)
    within = jnp.einsum(
        "hts,hsd->htd", attend_weights, value_heads, preferred_element_type=jnp.float32
    )
    query_scaled = (
        query_heads.astype(jnp.float32) * (jnp.exp(running) * scaling)[:, :, None]
    ).astype(jnp.bfloat16)
    within, query_scaled = lax.optimization_barrier((within, query_scaled))
    across = jnp.einsum(
        "htd,hde->hte",
        query_scaled,
        incoming.astype(jnp.bfloat16),
        preferred_element_type=jnp.float32,
    )
    unnormed = within + across
    spread = jnp.mean(unnormed * unnormed, axis=2, keepdims=True)
    normed = (
        (unnormed * lax.rsqrt(spread + 1e-06))
        .astype(jnp.bfloat16)
        .transpose(1, 0, 2)
        .reshape(length, model_width)
    )
    attended = jnp.dot(
        normed,
        lax.all_gather(out_weight, SEQ, axis=0, tiled=True),
        preferred_element_type=jnp.float32,
    )
    residual = (stream.astype(jnp.float32) + attended).astype(jnp.bfloat16)
    widened = residual.astype(jnp.float32)
    mixed_in = (
        widened * lax.rsqrt(jnp.mean(widened * widened, axis=1, keepdims=True) + 1e-06) * moe_gain
    ).astype(jnp.bfloat16)
    offsets = (token_index - device * length).reshape(-1)
    positions = jnp.arange(length)
    choose = (offsets[:, None] == positions[None, :]).astype(jnp.bfloat16)
    picked = jnp.dot(choose, mixed_in, preferred_element_type=jnp.float32).astype(jnp.bfloat16)
    picked = picked.reshape(token_index.shape + (model_width,))
    spread_weight = jnp.where(
        positions[:, None] == offsets[None, :], route_weight.reshape(-1)[None, :], 0.0
    ).reshape((length,) + token_index.shape)
    slots = token_index.shape[1]
    step = slots // CHUNKS
    total = widened
    for chunk in range(CHUNKS):
        window = slice(chunk * step, (chunk + 1) * step)
        arrived = lax.all_to_all(picked[:, window], SEQ, split_axis=0, concat_axis=0, tiled=True)
        gating = jnp.einsum(
            "snd,df->snf", arrived, gate_weight[0], preferred_element_type=jnp.float32
        )
        upward = jnp.einsum("snd,df->snf", arrived, up_weight[0], preferred_element_type=jnp.float32)
        activated = (jax.nn.silu(gating) * upward).astype(jnp.bfloat16)
        produced = jnp.einsum(
            "snf,fd->snd", activated, down_weight[0], preferred_element_type=jnp.float32
        ).astype(jnp.bfloat16)
        returned = lax.all_to_all(produced, SEQ, split_axis=0, concat_axis=0, tiled=True)
        remaining = spread_weight[:, :, window].reshape(length, -1)
        pieces = []
        for _ in range(SCATTER_PIECES):
            part = lax.reduce_precision(remaining, exponent_bits=8, mantissa_bits=7)
            pieces.append(part.astype(jnp.bfloat16))
            remaining = remaining - part
        pieces, returned = lax.optimization_barrier((pieces, returned))
        flat_returned = returned.reshape(-1, model_width)
        for part in pieces:
            total = total + jnp.dot(part, flat_returned, preferred_element_type=jnp.float32)
    return total.astype(jnp.bfloat16)


def solution(mesh):
    fine = jax.sharding.Mesh(
        mesh.devices.reshape(mesh.shape["dp"], 4, -1, 2),
        ("dp",) + SEQ,
    )
    placed = (
        P(("dp",) + SEQ, None),
        P(("dp",) + SEQ, None),
        P(("dp",) + SEQ, None),
        P(("dp",) + SEQ, None),
        P(("dp",) + SEQ, None),
        P("dp", SEQ),
        P("dp", SEQ),
        P(),
        P(SEQ, None),
        P(SEQ, None, None),
        P(SEQ, None, None),
        P(SEQ, None, None),
    )
    return jax.shard_map(
        shards, mesh=fine, in_specs=placed, out_specs=P(("dp",) + SEQ, None), check_vma=False
    )
```
